32 devices in a mesh: sect: 4 (over z), slab: 8 (over y, x, core).
Axes of the slice: x: 2, y: 2, z: 4, core: 2. Of those that a mesh axis runs over, the one named last changes fastest.
Arguments:
- vapor: float32 [30, 128, 4096], P(None, 'slab', 'sect'), may hold values from 0 to 0.05
- gas_temp: float32 [128, 4096], P('slab', 'sect'), may hold values from 1 to 2
- masses: float32 [30, 131072], P(None, ('sect', 'slab')), may hold values from 0.1 to 1
- drop_temp: float32 [131072], P(('sect', 'slab')), may hold values from 0.6 to 1.2
- cells: int32 [131072], P(('sect', 'slab')), may hold values from 0 to 65535
- flags: int32 [131072], P(('sect', 'slab')), may hold values 0 or 1
- moves: int32 [131072], P(('sect', 'slab')), may hold values from 0 to 2, as said below
- volat_a: float32 [30], replicated, may hold values from 1 to 3
- volat_b: float32 [30], replicated, may hold values from 1 to 4
- latent: float32 [30], replicated, may hold values from 0.5 to 5
Outputs:
- gas_next: float32 [31, 128, 4096], P(None, 'slab', 'sect')
- kept: float32 [31, 131072], P(None, ('sect', 'slab'))
- arrivals: float32 [31, 65536], P(None, ('sect', 'slab'))
The draws below stay inside these ranges and needn't reach their ends.
Inputs may be any that keep to these rules, and one draw needn't show every extreme that they name: In each device's 4096 parcels at most 1024 have moves 1 and at most 1024 have moves 2; some device has exactly 1024 with moves 1 and some device has exactly 1024 with moves 2.
All inputs are finite; a program needn't handle non-finite values. No bound on the sum of `flags` on one device may be relied on, other than what follows from the above.
Results may differ from the reference program's by a relative error of at most 0.0001.
Values sent between devices are 32-bit elements; how exact they have to be, the bound alone decides.
No kernel may reach another device: no remote copies, remote signals or barrier semaphores. Data moves between devices by JAX's collectives and lax.ppermute only.
A program may use at most 128 MiB of HBM per device.

```python
import math
import jax
import jax.numpy as jnp

NC = 30
CX = 16
P_DEV = 4096
RR_ITERS = 4
MOVE_CAP = 1024
FIELDS = 31
NX = 128
NYZ = 4096
P_TOTAL = 131072
N_SECT = 4
N_SLAB = 8


def draw_moves(key, part):
    blocks = P_TOTAL // P_DEV
    key_left, key_right, key_full, key_other, key_perm = jax.random.split(key, 5)
    left_count = jax.random.randint(key_left, (blocks,), 1, MOVE_CAP + 1)
    right_count = jax.random.randint(key_right, (blocks,), 1, MOVE_CAP + 1)
    full_left = jax.random.randint(key_full, (), 0, blocks)
    full_right = jax.random.randint(key_other, (), 0, blocks)
    block_ids = jnp.arange(blocks)
    left_count = jnp.where(block_ids == full_left, MOVE_CAP, left_count)
    right_count = jnp.where(block_ids == full_right, MOVE_CAP, right_count)
    ranks = jax.vmap(lambda sub: jax.random.permutation(sub, P_DEV))(jax.random.split(key_perm, blocks))
    moving = jnp.where(ranks < left_count[:, None], 1, jnp.where(ranks < (left_count + right_count)[:, None], 2, 0))
    return moving.reshape(-1).astype(jnp.int32)


def place_ends(values, key, least, largest):
    longest = values.shape.index(max(values.shape))
    spots = []
    for shift in (0, 1):
        where = [jax.random.randint(jax.random.fold_in(key, axis), (), 0, length) for axis, length in enumerate(values.shape)]
        where[longest] = (where[longest] + shift) % values.shape[longest]
        spots.append(tuple(where))
    return values.at[spots[0]].set(least).at[spots[1]].set(largest)


def levels(key, shape, shards, low, largest):
    gain = 1.0
    for position, parts in shards:
        draws = jax.random.uniform(jax.random.fold_in(jax.random.fold_in(key, 6), position), (parts,), jnp.float32, low / len(shards), largest / len(shards))
        gain = gain * jnp.repeat(jnp.exp(draws), shape[position] // parts).reshape((-1,) + (1,) * (len(shape) - 1 - position))
    return gain


def setup_inputs(seed: int = 0) -> dict:
    key_of = jax.random.split(jax.random.key(seed), 11)
    return {
        "vapor": jnp.clip(0.05 * jax.random.uniform(key_of[0], (NC, NX, NYZ), jnp.float32) ** levels(key_of[0], (NC, NX, NYZ), ((1, 8), (2, 4)), -0.2, 0.2), 0.0, 0.05),
        "gas_temp": jnp.clip(1.0 + 1.0 * jax.random.uniform(key_of[1], (NX, NYZ), jnp.float32) ** levels(key_of[1], (NX, NYZ), ((0, 8), (1, 4)), -0.2, 0.2), 1.0, 2.0),
        "masses": jnp.clip(jnp.exp(math.log(1.0) - 2.3025851 * jax.random.uniform(key_of[2], (NC, P_TOTAL), jnp.float32) ** levels(key_of[2], (NC, P_TOTAL), ((1, 32),), -0.2, 0.2)), 0.1, 1.0),
        "drop_temp": jnp.clip(0.6 + 0.6 * jax.random.uniform(key_of[3], (P_TOTAL,), jnp.float32) ** levels(key_of[3], (P_TOTAL,), ((0, 32),), -0.2, 0.2), 0.6, 1.2),
        "cells": place_ends(jax.random.randint(key_of[4], (P_TOTAL,), 0, CX * NYZ), jax.random.fold_in(key_of[4], 1), 0, (CX * NYZ) - 1).astype(jnp.int32),
        "flags": place_ends((jax.random.randint(key_of[5], (P_TOTAL,), 0, 2) < 1).astype(jnp.int32), jax.random.fold_in(key_of[5], 1), 0, 1),
        "moves": draw_moves(jax.random.fold_in(key_of[10], 71), 0),
        "volat_a": jnp.clip(jax.random.uniform(key_of[7], (NC,), jnp.float32, 1.0, 3.0), 1.0, 3.0),
        "volat_b": jnp.clip(jax.random.uniform(key_of[8], (NC,), jnp.float32, 1.0, 4.0), 1.0, 4.0),
        "latent": jnp.clip(jnp.exp(jax.random.uniform(key_of[9], (NC,), jnp.float32, math.log(0.5), math.log(5.0))), 0.5, 5.0),
    }


def parcel_update(masses, drop_temp, flags, vap_p, temp_p, volat_a, volat_b, latent):
    total = jnp.sum(masses, axis=0)
    frac = masses / total[None]
    surf = 0.5 * (drop_temp + temp_p)
    ratio = jnp.exp(volat_a[:, None] - volat_b[:, None] / surf[None])
    excess = ratio - 1.0
    share = jnp.full(total.shape, 0.5, jnp.float32)
    for sweep in range(RR_ITERS):
        denom = 1.0 + share[None] * excess
        residue = jnp.sum(frac * excess / denom, axis=0)
        slope = jnp.sum(frac * excess * excess / (denom * denom), axis=0) + 0.1
        share = jnp.clip(share + residue / slope, 0.02, 0.98)
    effect = flags.astype(jnp.float32) * share
    vap_eq = frac * ratio / (1.0 + effect[None] * excess)
    evap = 0.02 * total[None] * (vap_eq - vap_p)
    new_mass = masses - evap
    new_temp = drop_temp + 0.2 * (temp_p - drop_temp) - 0.5 * jnp.sum(latent[:, None] * evap, axis=0) / total
    heat = total * (drop_temp - temp_p)
    state = jnp.concatenate([new_mass, new_temp[None]], axis=0)
    terms = jnp.concatenate([0.1 * evap, 0.05 * heat[None]], axis=0)
    return state, terms


def stencil(gas):
    padded = jnp.pad(gas, ((0, 0), (1, 1), (0, 0)))
    down = padded[:, :-2]
    upper = padded[:, 2:]
    return gas + 0.2 * (upper - 2.0 * gas + down) - 0.3 * (gas - down)


def pack_slots(state, chosen):
    blocks = chosen.shape[0]
    slot = jnp.cumsum(chosen.astype(jnp.int32), axis=1) - 1
    slot = jnp.where(chosen, slot, MOVE_CAP).astype(jnp.int32)
    block_ids = jnp.broadcast_to(jnp.arange(blocks, dtype=jnp.int32)[:, None], slot.shape)
    values = jnp.transpose(state.reshape(FIELDS, blocks, P_DEV), (1, 2, 0))
    buffer = jnp.zeros((blocks, MOVE_CAP, FIELDS), jnp.float32)
    return buffer.at[block_ids, slot].set(values, mode="drop")


def reference(vapor, gas_temp, masses, drop_temp, cells, flags, moves, volat_a, volat_b, latent):
    gas = jnp.concatenate([vapor, gas_temp[None]], axis=0)
    slab_cells = CX * NYZ
    gas_slabs = gas.reshape(FIELDS, N_SLAB, slab_cells)
    slab_of = ((jnp.arange(P_TOTAL, dtype=jnp.int32) // P_DEV) % N_SLAB).astype(jnp.int32)
    at_parcel = gas_slabs[:, slab_of, cells]
    state, terms = parcel_update(masses, drop_temp, flags, at_parcel[:NC], at_parcel[NC], volat_a, volat_b, latent)
    segment_ids = (slab_of * slab_cells + cells).astype(jnp.int32)
    source = jax.ops.segment_sum(terms.T, segment_ids, N_SLAB * slab_cells).T.reshape(FIELDS, NX, NYZ)
    gas_next = stencil(gas) + source
    kept = jnp.where(moves[None] == 0, state, 0.0)
    blocks = N_SECT * N_SLAB
    block_moves = moves.reshape(blocks, P_DEV)
    left_buf = pack_slots(state, block_moves == 1).reshape(N_SECT, N_SLAB, MOVE_CAP, FIELDS)
    right_buf = pack_slots(state, block_moves == 2).reshape(N_SECT, N_SLAB, MOVE_CAP, FIELDS)
    zero_slab = jnp.zeros((N_SECT, 1, MOVE_CAP, FIELDS), jnp.float32)
    from_prev = jnp.concatenate([zero_slab, right_buf[:, :-1]], axis=1)
    from_next = jnp.concatenate([left_buf[:, 1:], zero_slab], axis=1)
    joined = jnp.concatenate([from_prev, from_next], axis=2)
    arrivals = jnp.transpose(joined, (3, 0, 1, 2)).reshape(FIELDS, blocks * 2 * MOVE_CAP)
    return gas_next, kept, arrivals
```

```python
import jax
import jax.numpy as jnp
from jax import lax
from jax.experimental import pallas as pl
from jax.experimental.pallas import tpu as pltpu
from jax.sharding import PartitionSpec as P

NC = 30
RR_ITERS = 4
MOVE_CAP = 1024
UNROLL = 8


def with_halo(block, sides, width):
    for axis, dim in sides:
        count = lax.axis_size(axis)
        forward = [(i, i + 1) for i in range(count - 1)]
        backward = [(target, source) for source, target in forward]
        low = lax.ppermute(
            lax.slice_in_dim(block, block.shape[dim] - width, None, axis=dim), axis, forward
        )
        high = lax.ppermute(lax.slice_in_dim(block, 0, width, axis=dim), axis, backward)
        block = jnp.concatenate([low, block, high], axis=dim)
    return block


def shifted(shard, axis, by):
    length = lax.axis_size(axis)
    pairs = [(i, i + by) for i in range(length) if 0 <= i + by < length]
    return lax.ppermute(shard, axis, pairs)


def parcel_update(masses, drop_temp, flags, vap_p, temp_p, volat_a, volat_b, latent):
    total = jnp.sum(masses, axis=0)
    frac = masses / total[None]
    surf = 0.5 * (drop_temp + temp_p)
    ratio = jnp.exp(volat_a[:, None] - volat_b[:, None] / surf[None])
    excess = ratio - 1.0
    share = jnp.full(total.shape, 0.5, jnp.float32)
    for sweep in range(RR_ITERS):
        denom = 1.0 + share[None] * excess
        residue = jnp.sum(frac * excess / denom, axis=0)
        slope = jnp.sum(frac * excess * excess / (denom * denom), axis=0) + 0.1
        share = jnp.clip(share + residue / slope, 0.02, 0.98)
    effect = flags.astype(jnp.float32) * share
    vap_eq = frac * ratio / (1.0 + effect[None] * excess)
    evap = 0.02 * total[None] * (vap_eq - vap_p)
    new_mass = masses - evap
    new_temp = (
        drop_temp
        + 0.2 * (temp_p - drop_temp)
        - 0.5 * jnp.sum(latent[:, None] * evap, axis=0) / total
    )
    heat = total * (drop_temp - temp_p)
    state = jnp.concatenate([new_mass, new_temp[None]], axis=0)
    terms = jnp.concatenate([0.1 * evap, 0.05 * heat[None]], axis=0)
    return (state, terms)


def pack_slots(state, chosen):
    slot = jnp.cumsum(chosen.astype(jnp.int32)) - 1
    slot = jnp.where(chosen, slot, MOVE_CAP)
    buffer = jnp.zeros((MOVE_CAP, state.shape[0]), jnp.float32)
    return buffer.at[slot].set(state.T, mode="drop").T


def _gather_kernel(count_ref, order_ref, local_ref, table_ref, out_ref):
    out_ref[...] = jnp.zeros(out_ref.shape, out_ref.dtype)

    def step(i, carry):
        base = i * UNROLL
        for j in range(UNROLL):
            p = order_ref[base + j]
            out_ref[pl.ds(p, 1), :] = table_ref[pl.ds(local_ref[p], 1), :]
        return carry

    lax.fori_loop(0, (count_ref[0] + UNROLL - 1) // UNROLL, step, 0)


def _scatter_kernel(count_ref, order_ref, seg_ref, rows_ref, out_ref, acc_ref):
    acc_ref[...] = jnp.zeros(acc_ref.shape, acc_ref.dtype)

    def step(i, carry):
        base = i * UNROLL
        for j in range(UNROLL):
            p = order_ref[base + j]
            s = seg_ref[p]
            acc_ref[pl.ds(s, 1), :] += rows_ref[pl.ds(p, 1), :]
        return carry

    lax.fori_loop(0, (count_ref[0] + UNROLL - 1) // UNROLL, step, 0)
    out_ref[...] = acc_ref[pl.ds(0, out_ref.shape[0]), :]


def row_gather(count, order, local, table):
    n_out = order.shape[0]
    n_tab, width = table.shape
    spec = pltpu.PrefetchScalarGridSpec(
        num_scalar_prefetch=3,
        grid=(1,),
        in_specs=[pl.BlockSpec((n_tab, width), lambda i, *_: (0, 0))],
        out_specs=pl.BlockSpec((n_out, width), lambda i, *_: (0, 0)),
    )
    return pl.pallas_call(
        _gather_kernel,
        grid_spec=spec,
        out_shape=jax.ShapeDtypeStruct((n_out, width), table.dtype),
    )(count, order, local, table)


def row_scatter_add(count, order, seg, rows, n_cells):
    n_rows, width = rows.shape
    spec = pltpu.PrefetchScalarGridSpec(
        num_scalar_prefetch=3,
        grid=(1,),
        in_specs=[pl.BlockSpec((n_rows, width), lambda i, *_: (0, 0))],
        out_specs=pl.BlockSpec((n_cells, width), lambda i, *_: (0, 0)),
        scratch_shapes=[pltpu.VMEM((n_cells + UNROLL, width), jnp.float32)],
    )
    return pl.pallas_call(
        _scatter_kernel,
        grid_spec=spec,
        out_shape=jax.ShapeDtypeStruct((n_cells, width), rows.dtype),
    )(count, order, seg, rows)


def body(vapor, gas_temp, masses, drop_temp, cells, flags, moves, volat_a, volat_b, latent):
    gas_block = jnp.concatenate([vapor, gas_temp[None]], axis=0)
    fields, width_x, width_yz = gas_block.shape
    n_cells = width_x * width_yz
    sections = lax.axis_size("sect")
    own_sect = lax.axis_index("sect")
    plane = sections * width_yz
    all_cells = lax.all_gather(cells, "sect", axis=0, tiled=True)
    n_all = all_cells.shape[0]
    cell_row = all_cells // plane
    cell_col = all_cells % plane
    owned = (cell_col // width_yz) == own_sect
    local_cell = (cell_row * width_yz + cell_col % width_yz).astype(jnp.int32)
    seg = jnp.where(owned, local_cell, n_cells).astype(jnp.int32)
    position = jnp.arange(n_all, dtype=jnp.int32)
    order = lax.sort(jnp.where(owned, 0, n_all).astype(jnp.int32) + position) % n_all
    count = jnp.sum(owned.astype(jnp.int32)).reshape(1)
    table = gas_block.reshape(fields, n_cells).T
    picked = jnp.where(owned[None, :], row_gather(count, order, local_cell, table).T, 0.0)
    at_parcel = lax.psum_scatter(picked, "sect", scatter_dimension=1, tiled=True)
    state, terms = parcel_update(
        masses, drop_temp, flags, at_parcel[:NC], at_parcel[NC], volat_a, volat_b, latent
    )
    padded = with_halo(gas_block, (("slab", 1),), 1)
    down = padded[:, :-2]
    upper = padded[:, 2:]
    flowed = gas_block + 0.2 * (upper - 2.0 * gas_block + down) - 0.3 * (gas_block - down)
    all_terms = lax.all_gather(terms, "sect", axis=1, tiled=True)
    summed = row_scatter_add(count, order, seg, all_terms.T, n_cells)
    source = summed.T.reshape(fields, width_x, width_yz)
    gas_next = flowed + source
    kept = jnp.where(moves[None] == 0, state, 0.0)
    from_prev = shifted(pack_slots(state, moves == 2), "slab", 1)
    from_next = shifted(pack_slots(state, moves == 1), "slab", -1)
    arrivals = jnp.concatenate([from_prev, from_next], axis=1)
    return (gas_next, kept, arrivals)


def solution(mesh):
    in_specs = (
        P(None, "slab", "sect"),
        P("slab", "sect"),
        P(None, ("sect", "slab")),
        P(("sect", "slab")),
        P(("sect", "slab")),
        P(("sect", "slab")),
        P(("sect", "slab")),
        P(),
        P(),
        P(),
    )
    out_specs = (P(None, "slab", "sect"), P(None, ("sect", "slab")), P(None, ("sect", "slab")))
    return jax.shard_map(body, mesh=mesh, in_specs=in_specs, out_specs=out_specs, check_vma=False)
```

```python
import jax
import jax.numpy as jnp
from jax import lax
from jax.experimental import pallas as pl
from jax.experimental.pallas import tpu as pltpu
from jax.experimental.layout import Layout, with_layout_constraint
from jax.sharding import PartitionSpec as P

NC = 30
RR_ITERS = 4
MOVE_CAP = 1024
UNROLL = 8


def with_halo(block, sides, width):
    for axis, dim in sides:
        count = lax.axis_size(axis)
        forward = [(i, i + 1) for i in range(count - 1)]
        backward = [(target, source) for source, target in forward]
        low = lax.ppermute(
            lax.slice_in_dim(block, block.shape[dim] - width, None, axis=dim), axis, forward
        )
        high = lax.ppermute(lax.slice_in_dim(block, 0, width, axis=dim), axis, backward)
        block = jnp.concatenate([low, block, high], axis=dim)
    return block


def shifted(shard, axis, by):
    length = lax.axis_size(axis)
    pairs = [(i, i + by) for i in range(length) if 0 <= i + by < length]
    return lax.ppermute(shard, axis, pairs)


def parcel_update(masses, drop_temp, flags, vap_p, temp_p, volat_a, volat_b, latent):
    total = jnp.sum(masses, axis=0)
    frac = masses / total[None]
    surf = 0.5 * (drop_temp + temp_p)
    ratio = jnp.exp(volat_a[:, None] - volat_b[:, None] / surf[None])
    excess = ratio - 1.0
    share = jnp.full(total.shape, 0.5, jnp.float32)
    for sweep in range(RR_ITERS):
        denom = 1.0 + share[None] * excess
        residue = jnp.sum(frac * excess / denom, axis=0)
        slope = jnp.sum(frac * excess * excess / (denom * denom), axis=0) + 0.1
        share = jnp.clip(share + residue / slope, 0.02, 0.98)
    effect = flags.astype(jnp.float32) * share
    vap_eq = frac * ratio / (1.0 + effect[None] * excess)
    evap = 0.02 * total[None] * (vap_eq - vap_p)
    new_mass = masses - evap
    new_temp = (
        drop_temp
        + 0.2 * (temp_p - drop_temp)
        - 0.5 * jnp.sum(latent[:, None] * evap, axis=0) / total
    )
    heat = total * (drop_temp - temp_p)
    state = jnp.concatenate([new_mass, new_temp[None]], axis=0)
    terms = jnp.concatenate([0.1 * evap, 0.05 * heat[None]], axis=0)
    return (state, terms)


def pack_slots(state, chosen):
    slot = jnp.cumsum(chosen.astype(jnp.int32)) - 1
    slot = jnp.where(chosen, slot, MOVE_CAP)
    buffer = jnp.zeros((MOVE_CAP, state.shape[0]), jnp.float32)
    return buffer.at[slot].set(state.T, mode="drop").T


def _gather_kernel(count_ref, order_ref, local_ref, table_ref, out_ref):
    out_ref[...] = jnp.zeros(out_ref.shape, out_ref.dtype)

    def step(i, carry):
        base = i * UNROLL
        for j in range(UNROLL):
            p = order_ref[base + j]
            out_ref[pl.ds(p, 1), :] = table_ref[pl.ds(local_ref[p], 1), :]
        return carry

    lax.fori_loop(0, (count_ref[0] + UNROLL - 1) // UNROLL, step, 0)


def _scatter_kernel(count_ref, order_ref, seg_ref, rows_ref, out_ref, acc_ref):
    acc_ref[...] = jnp.zeros(acc_ref.shape, acc_ref.dtype)

    def step(i, carry):
        base = i * UNROLL
        for j in range(UNROLL):
            p = order_ref[base + j]
            s = seg_ref[p]
            acc_ref[pl.ds(s, 1), :] += rows_ref[pl.ds(p, 1), :]
        return carry

    lax.fori_loop(0, (count_ref[0] + UNROLL - 1) // UNROLL, step, 0)
    out_ref[...] = acc_ref[pl.ds(0, out_ref.shape[0]), :]


def row_gather(count, order, local, table):
    n_out = order.shape[0]
    n_tab, width = table.shape
    spec = pltpu.PrefetchScalarGridSpec(
        num_scalar_prefetch=3,
        grid=(1,),
        in_specs=[pl.BlockSpec((n_tab, width), lambda i, *_: (0, 0))],
        out_specs=pl.BlockSpec((n_out, width), lambda i, *_: (0, 0)),
    )
    return pl.pallas_call(
        _gather_kernel,
        grid_spec=spec,
        out_shape=jax.ShapeDtypeStruct((n_out, width), table.dtype),
    )(count, order, local, table)


def row_scatter_add(count, order, seg, rows, n_cells):
    n_rows, width = rows.shape
    spec = pltpu.PrefetchScalarGridSpec(
        num_scalar_prefetch=3,
        grid=(1,),
        in_specs=[pl.BlockSpec((n_rows, width), lambda i, *_: (0, 0))],
        out_specs=pl.BlockSpec((n_cells, width), lambda i, *_: (0, 0)),
        scratch_shapes=[pltpu.VMEM((n_cells + UNROLL, width), jnp.float32)],
    )
    return pl.pallas_call(
        _scatter_kernel,
        grid_spec=spec,
        out_shape=jax.ShapeDtypeStruct((n_cells, width), rows.dtype),
    )(count, order, seg, rows)


def body(vapor, gas_temp, masses, drop_temp, cells, flags, moves, volat_a, volat_b, latent):
    gas_block = jnp.concatenate([vapor, gas_temp[None]], axis=0)
    fields, width_x, width_yz = gas_block.shape
    n_cells = width_x * width_yz
    sections = lax.axis_size("sect")
    own_sect = lax.axis_index("sect")
    plane = sections * width_yz
    all_cells = lax.all_gather(cells, "sect", axis=0, tiled=True)
    n_all = all_cells.shape[0]
    cell_row = all_cells // plane
    cell_col = all_cells % plane
    owned = (cell_col // width_yz) == own_sect
    local_cell = (cell_row * width_yz + cell_col % width_yz).astype(jnp.int32)
    seg = jnp.where(owned, local_cell, n_cells).astype(jnp.int32)
    position = jnp.arange(n_all, dtype=jnp.int32)
    order = lax.sort(jnp.where(owned, 0, n_all).astype(jnp.int32) + position) % n_all
    count = jnp.sum(owned.astype(jnp.int32)).reshape(1)
    table = gas_block.reshape(fields, n_cells).T
    picked = jnp.where(owned[None, :], row_gather(count, order, local_cell, table).T, 0.0)
    picked = with_layout_constraint(picked, Layout(major_to_minor=(0, 1)))
    at_parcel = lax.psum_scatter(picked, "sect", scatter_dimension=1, tiled=True)
    at_parcel = with_layout_constraint(at_parcel, Layout(major_to_minor=(0, 1)))
    state, terms = parcel_update(
        masses, drop_temp, flags, at_parcel[:NC], at_parcel[NC], volat_a, volat_b, latent
    )
    padded = with_halo(gas_block, (("slab", 1),), 1)
    down = padded[:, :-2]
    upper = padded[:, 2:]
    flowed = gas_block + 0.2 * (upper - 2.0 * gas_block + down) - 0.3 * (gas_block - down)
    terms = with_layout_constraint(terms, Layout(major_to_minor=(0, 1)))
    all_terms = lax.all_gather(terms, "sect", axis=1, tiled=True)
    all_terms = with_layout_constraint(all_terms, Layout(major_to_minor=(0, 1)))
    summed = row_scatter_add(count, order, seg, all_terms.T, n_cells)
    source = summed.T.reshape(fields, width_x, width_yz)
    gas_next = flowed + source
    kept = jnp.where(moves[None] == 0, state, 0.0)
    from_prev = shifted(pack_slots(state, moves == 2), "slab", 1)
    from_next = shifted(pack_slots(state, moves == 1), "slab", -1)
    arrivals = jnp.concatenate([from_prev, from_next], axis=1)
    return (gas_next, kept, arrivals)


def solution(mesh):
    in_specs = (
        P(None, "slab", "sect"),
        P("slab", "sect"),
        P(None, ("sect", "slab")),
        P(("sect", "slab")),
        P(("sect", "slab")),
        P(("sect", "slab")),
        P(("sect", "slab")),
        P(),
        P(),
        P(),
    )
    out_specs = (P(None, "slab", "sect"), P(None, ("sect", "slab")), P(None, ("sect", "slab")))
    return jax.shard_map(body, mesh=mesh, in_specs=in_specs, out_specs=out_specs, check_vma=False)
```

```python
import jax
import jax.numpy as jnp
from jax import lax
from jax.experimental import pallas as pl
from jax.experimental.pallas import tpu as pltpu
from jax.experimental.layout import Layout, with_layout_constraint
from jax.sharding import PartitionSpec as P

NC = 30
RR_ITERS = 4
MOVE_CAP = 1024
UNROLL = 8


def with_halo(block, sides, width):
    for axis, dim in sides:
        count = lax.axis_size(axis)
        forward = [(i, i + 1) for i in range(count - 1)]
        backward = [(target, source) for source, target in forward]
        low = lax.ppermute(
            lax.slice_in_dim(block, block.shape[dim] - width, None, axis=dim), axis, forward
        )
        high = lax.ppermute(lax.slice_in_dim(block, 0, width, axis=dim), axis, backward)
        block = jnp.concatenate([low, block, high], axis=dim)
    return block


def shifted(shard, axis, by):
    length = lax.axis_size(axis)
    pairs = [(i, i + by) for i in range(length) if 0 <= i + by < length]
    return lax.ppermute(shard, axis, pairs)


def parcel_update(masses, drop_temp, flags, vap_p, temp_p, volat_a, volat_b, latent):
    total = jnp.sum(masses, axis=0)
    frac = masses / total[None]
    surf = 0.5 * (drop_temp + temp_p)
    ratio = jnp.exp(volat_a[:, None] - volat_b[:, None] / surf[None])
    excess = ratio - 1.0
    share = jnp.full(total.shape, 0.5, jnp.float32)
    for sweep in range(RR_ITERS):
        denom = 1.0 + share[None] * excess
        residue = jnp.sum(frac * excess / denom, axis=0)
        slope = jnp.sum(frac * excess * excess / (denom * denom), axis=0) + 0.1
        share = jnp.clip(share + residue / slope, 0.02, 0.98)
    effect = flags.astype(jnp.float32) * share
    vap_eq = frac * ratio / (1.0 + effect[None] * excess)
    evap = 0.02 * total[None] * (vap_eq - vap_p)
    new_mass = masses - evap
    new_temp = (
        drop_temp
        + 0.2 * (temp_p - drop_temp)
        - 0.5 * jnp.sum(latent[:, None] * evap, axis=0) / total
    )
    heat = total * (drop_temp - temp_p)
    state = jnp.concatenate([new_mass, new_temp[None]], axis=0)
    terms = jnp.concatenate([0.1 * evap, 0.05 * heat[None]], axis=0)
    return (state, terms)


def pack_slots(state, chosen):
    slot = jnp.where(chosen, jnp.cumsum(chosen.astype(jnp.int32)) - 1, -1)
    onehot = (slot[:, None] == jnp.arange(MOVE_CAP, dtype=jnp.int32)[None, :]).astype(jnp.bfloat16)
    high = lax.reduce_precision(state, exponent_bits=8, mantissa_bits=7)
    rest = state - high
    middle = lax.reduce_precision(rest, exponent_bits=8, mantissa_bits=7)
    low = rest - middle
    parts = jnp.concatenate([high, middle, low], axis=0).astype(jnp.bfloat16)
    out = jnp.dot(parts, onehot, preferred_element_type=jnp.float32)
    rows = state.shape[0]
    return (out[:rows] + out[rows : 2 * rows]) + out[2 * rows :]


def _gather_kernel(count_ref, order_ref, local_ref, table_ref, out_ref):
    out_ref[...] = jnp.zeros(out_ref.shape, out_ref.dtype)

    def step(i, carry):
        base = i * UNROLL
        for j in range(UNROLL):
            p = order_ref[base + j]
            out_ref[pl.ds(p, 1), :] = table_ref[pl.ds(local_ref[p], 1), :]
        return carry

    lax.fori_loop(0, (count_ref[0] + UNROLL - 1) // UNROLL, step, 0)


def _scatter_kernel(count_ref, order_ref, seg_ref, rows_ref, out_ref, acc_ref):
    acc_ref[...] = jnp.zeros(acc_ref.shape, acc_ref.dtype)

    def step(i, carry):
        base = i * UNROLL
        for j in range(UNROLL):
            p = order_ref[base + j]
            s = seg_ref[p]
            acc_ref[pl.ds(s, 1), :] += rows_ref[pl.ds(p, 1), :]
        return carry

    lax.fori_loop(0, (count_ref[0] + UNROLL - 1) // UNROLL, step, 0)
    out_ref[...] = acc_ref[pl.ds(0, out_ref.shape[0]), :]


def row_gather(count, order, local, table):
    n_out = order.shape[0]
    n_tab, width = table.shape
    spec = pltpu.PrefetchScalarGridSpec(
        num_scalar_prefetch=3,
        grid=(1,),
        in_specs=[pl.BlockSpec((n_tab, width), lambda i, *_: (0, 0))],
        out_specs=pl.BlockSpec((n_out, width), lambda i, *_: (0, 0)),
    )
    return pl.pallas_call(
        _gather_kernel,
        grid_spec=spec,
        out_shape=jax.ShapeDtypeStruct((n_out, width), table.dtype),
    )(count, order, local, table)


def row_scatter_add(count, order, seg, rows, n_cells):
    n_rows, width = rows.shape
    spec = pltpu.PrefetchScalarGridSpec(
        num_scalar_prefetch=3,
        grid=(1,),
        in_specs=[pl.BlockSpec((n_rows, width), lambda i, *_: (0, 0))],
        out_specs=pl.BlockSpec((n_cells, width), lambda i, *_: (0, 0)),
        scratch_shapes=[pltpu.VMEM((n_cells + UNROLL, width), jnp.float32)],
    )
    return pl.pallas_call(
        _scatter_kernel,
        grid_spec=spec,
        out_shape=jax.ShapeDtypeStruct((n_cells, width), rows.dtype),
    )(count, order, seg, rows)


def body(vapor, gas_temp, masses, drop_temp, cells, flags, moves, volat_a, volat_b, latent):
    gas_block = jnp.concatenate([vapor, gas_temp[None]], axis=0)
    fields, width_x, width_yz = gas_block.shape
    n_cells = width_x * width_yz
    sections = lax.axis_size("sect")
    own_sect = lax.axis_index("sect")
    plane = sections * width_yz
    all_cells = lax.all_gather(cells.astype(jnp.float32), "sect", axis=0, tiled=True)
    all_cells = all_cells.astype(jnp.int32)
    n_all = all_cells.shape[0]
    cell_row = all_cells // plane
    cell_col = all_cells % plane
    owned = (cell_col // width_yz) == own_sect
    local_cell = (cell_row * width_yz + cell_col % width_yz).astype(jnp.int32)
    seg = jnp.where(owned, local_cell, n_cells).astype(jnp.int32)
    position = jnp.arange(n_all, dtype=jnp.int32)
    order = lax.sort(jnp.where(owned, 0, n_all).astype(jnp.int32) + position) % n_all
    count = jnp.sum(owned.astype(jnp.int32)).reshape(1)
    table = gas_block.reshape(fields, n_cells).T
    picked = jnp.where(owned[None, :], row_gather(count, order, local_cell, table).T, 0.0)
    picked = with_layout_constraint(picked, Layout(major_to_minor=(0, 1)))
    at_parcel = lax.psum_scatter(picked, "sect", scatter_dimension=1, tiled=True)
    at_parcel = with_layout_constraint(at_parcel, Layout(major_to_minor=(0, 1)))
    state, terms = parcel_update(
        masses, drop_temp, flags, at_parcel[:NC], at_parcel[NC], volat_a, volat_b, latent
    )
    padded = with_halo(gas_block, (("slab", 1),), 1)
    down = padded[:, :-2]
    upper = padded[:, 2:]
    flowed = gas_block + 0.2 * (upper - 2.0 * gas_block + down) - 0.3 * (gas_block - down)
    terms = with_layout_constraint(terms, Layout(major_to_minor=(0, 1)))
    all_terms = lax.all_gather(terms, "sect", axis=1, tiled=True)
    all_terms = with_layout_constraint(all_terms, Layout(major_to_minor=(0, 1)))
    summed = row_scatter_add(count, order, seg, all_terms.T, n_cells)
    source = summed.T.reshape(fields, width_x, width_yz)
    gas_next = flowed + source
    kept = jnp.where(moves[None] == 0, state, 0.0)
    from_prev = shifted(pack_slots(state, moves == 2), "slab", 1)
    from_next = shifted(pack_slots(state, moves == 1), "slab", -1)
    arrivals = jnp.concatenate([from_prev, from_next], axis=1)
    return (gas_next, kept, arrivals)


def solution(mesh):
    in_specs = (
        P(None, "slab", "sect"),
        P("slab", "sect"),
        P(None, ("sect", "slab")),
        P(("sect", "slab")),
        P(("sect", "slab")),
        P(("sect", "slab")),
        P(("sect", "slab")),
        P(),
        P(),
        P(),
    )
    out_specs = (P(None, "slab", "sect"), P(None, ("sect", "slab")), P(None, ("sect", "slab")))
    return jax.shard_map(body, mesh=mesh, in_specs=in_specs, out_specs=out_specs, check_vma=False)
```

```python
import jax
import jax.numpy as jnp
from jax import lax
from jax.experimental import pallas as pl
from jax.experimental.pallas import tpu as pltpu
from jax.experimental.layout import Layout, with_layout_constraint
from jax.sharding import PartitionSpec as P

NC = 30
RR_ITERS = 4
MOVE_CAP = 1024
UNROLL = 8


def with_halo(block, sides, width):
    for axis, dim in sides:
        count = lax.axis_size(axis)
        forward = [(i, i + 1) for i in range(count - 1)]
        backward = [(target, source) for source, target in forward]
        low = lax.ppermute(
            lax.slice_in_dim(block, block.shape[dim] - width, None, axis=dim), axis, forward
        )
        high = lax.ppermute(lax.slice_in_dim(block, 0, width, axis=dim), axis, backward)
        block = jnp.concatenate([low, block, high], axis=dim)
    return block


def shifted(shard, axis, by):
    length = lax.axis_size(axis)
    pairs = [(i, i + by) for i in range(length) if 0 <= i + by < length]
    return lax.ppermute(shard, axis, pairs)


def parcel_update(masses, drop_temp, flags, vap_p, temp_p, volat_a, volat_b, latent):
    total = jnp.sum(masses, axis=0)
    frac = masses / total[None]
    surf = 0.5 * (drop_temp + temp_p)
    ratio = jnp.exp(volat_a[:, None] - volat_b[:, None] / surf[None])
    excess = ratio - 1.0
    share = jnp.full(total.shape, 0.5, jnp.float32)
    for sweep in range(RR_ITERS):
        denom = 1.0 + share[None] * excess
        residue = jnp.sum(frac * excess / denom, axis=0)
        slope = jnp.sum(frac * excess * excess / (denom * denom), axis=0) + 0.1
        share = jnp.clip(share + residue / slope, 0.02, 0.98)
    effect = flags.astype(jnp.float32) * share
    vap_eq = frac * ratio / (1.0 + effect[None] * excess)
    evap = 0.02 * total[None] * (vap_eq - vap_p)
    new_mass = masses - evap
    new_temp = (
        drop_temp
        + 0.2 * (temp_p - drop_temp)
        - 0.5 * jnp.sum(latent[:, None] * evap, axis=0) / total
    )
    heat = total * (drop_temp - temp_p)
    state = jnp.concatenate([new_mass, new_temp[None]], axis=0)
    terms = jnp.concatenate([0.1 * evap, 0.05 * heat[None]], axis=0)
    return (state, terms)


def pack_slots(state, chosen):
    slot = jnp.where(chosen, jnp.cumsum(chosen.astype(jnp.int32)) - 1, -1)
    onehot = (slot[:, None] == jnp.arange(MOVE_CAP, dtype=jnp.int32)[None, :]).astype(jnp.bfloat16)
    high = lax.reduce_precision(state, exponent_bits=8, mantissa_bits=7)
    rest = state - high
    middle = lax.reduce_precision(rest, exponent_bits=8, mantissa_bits=7)
    low = rest - middle
    parts = jnp.concatenate([high, middle, low], axis=0).astype(jnp.bfloat16)
    out = jnp.dot(parts, onehot, preferred_element_type=jnp.float32)
    rows = state.shape[0]
    return (out[:rows] + out[rows : 2 * rows]) + out[2 * rows :]


def _gather_kernel(count_ref, order_ref, local_ref, table_ref, out_ref):
    out_ref[...] = jnp.zeros(out_ref.shape, out_ref.dtype)

    def step(i, carry):
        base = i * UNROLL
        for j in range(UNROLL):
            p = order_ref[base + j]
            out_ref[pl.ds(p, 1), :] = table_ref[pl.ds(local_ref[p], 1), :]
        return carry

    lax.fori_loop(0, (count_ref[0] + UNROLL - 1) // UNROLL, step, 0)


def _scatter_kernel(count_ref, order_ref, seg_ref, rows_ref, out_ref, acc_ref):
    acc_ref[...] = jnp.zeros(acc_ref.shape, acc_ref.dtype)

    def step(i, carry):
        base = i * UNROLL
        for j in range(UNROLL):
            p = order_ref[base + j]
            s = seg_ref[p]
            acc_ref[pl.ds(s, 1), :] += rows_ref[pl.ds(p, 1), :]
        return carry

    lax.fori_loop(0, (count_ref[0] + UNROLL - 1) // UNROLL, step, 0)
    out_ref[...] = acc_ref[pl.ds(0, out_ref.shape[0]), :]


def row_gather(count, order, local, table):
    n_out = order.shape[0]
    n_tab, width = table.shape
    spec = pltpu.PrefetchScalarGridSpec(
        num_scalar_prefetch=3,
        grid=(1,),
        in_specs=[pl.BlockSpec((n_tab, width), lambda i, *_: (0, 0))],
        out_specs=pl.BlockSpec((n_out, width), lambda i, *_: (0, 0)),
    )
    return pl.pallas_call(
        _gather_kernel,
        grid_spec=spec,
        out_shape=jax.ShapeDtypeStruct((n_out, width), table.dtype),
    )(count, order, local, table)


def row_scatter_add(count, order, seg, rows, n_cells):
    n_rows, width = rows.shape
    spec = pltpu.PrefetchScalarGridSpec(
        num_scalar_prefetch=3,
        grid=(1,),
        in_specs=[pl.BlockSpec((n_rows, width), lambda i, *_: (0, 0))],
        out_specs=pl.BlockSpec((n_cells, width), lambda i, *_: (0, 0)),
        scratch_shapes=[pltpu.VMEM((n_cells + UNROLL, width), jnp.float32)],
    )
    return pl.pallas_call(
        _scatter_kernel,
        grid_spec=spec,
        out_shape=jax.ShapeDtypeStruct((n_cells, width), rows.dtype),
    )(count, order, seg, rows)


def field_major(x):
    return with_layout_constraint(x, Layout(major_to_minor=(0, 1)))


def body(vapor, gas_temp, masses, drop_temp, cells, flags, moves, volat_a, volat_b, latent):
    gas_block = jnp.concatenate([vapor, gas_temp[None]], axis=0)
    fields, width_x, width_yz = gas_block.shape
    n_cells = width_x * width_yz
    sections = lax.axis_size("sect")
    own_sect = lax.axis_index("sect")
    plane = sections * width_yz
    parcel_in = jnp.concatenate(
        [masses, drop_temp[None], flags.astype(jnp.float32)[None]], axis=0
    )
    all_in = field_major(lax.all_gather(field_major(parcel_in), "sect", axis=1, tiled=True))
    all_cells = lax.all_gather(cells.astype(jnp.float32), "sect", axis=0, tiled=True)
    all_cells = all_cells.astype(jnp.int32)
    n_all = all_cells.shape[0]
    cell_row = all_cells // plane
    cell_col = all_cells % plane
    owned = (cell_col // width_yz) == own_sect
    local_cell = (cell_row * width_yz + cell_col % width_yz).astype(jnp.int32)
    seg = jnp.where(owned, local_cell, n_cells).astype(jnp.int32)
    position = jnp.arange(n_all, dtype=jnp.int32)
    order = lax.sort(jnp.where(owned, 0, n_all).astype(jnp.int32) + position) % n_all
    count = jnp.sum(owned.astype(jnp.int32)).reshape(1)
    table = gas_block.reshape(fields, n_cells).T
    at_parcel = jnp.where(owned[None, :], row_gather(count, order, local_cell, table).T, 0.0)
    state_all, terms_all = parcel_update(
        all_in[:NC], all_in[NC], all_in[NC + 1], at_parcel[:NC], at_parcel[NC],
        volat_a, volat_b, latent,
    )
    state_own = field_major(jnp.where(owned[None, :], state_all, 0.0))
    state = field_major(lax.psum_scatter(state_own, "sect", scatter_dimension=1, tiled=True))
    padded = with_halo(gas_block, (("slab", 1),), 1)
    down = padded[:, :-2]
    upper = padded[:, 2:]
    flowed = gas_block + 0.2 * (upper - 2.0 * gas_block + down) - 0.3 * (gas_block - down)
    summed = row_scatter_add(count, order, seg, terms_all.T, n_cells)
    source = summed.T.reshape(fields, width_x, width_yz)
    gas_next = flowed + source
    kept = jnp.where(moves[None] == 0, state, 0.0)
    from_prev = shifted(pack_slots(state, moves == 2), "slab", 1)
    from_next = shifted(pack_slots(state, moves == 1), "slab", -1)
    arrivals = jnp.concatenate([from_prev, from_next], axis=1)
    return (gas_next, kept, arrivals)


def solution(mesh):
    in_specs = (
        P(None, "slab", "sect"),
        P("slab", "sect"),
        P(None, ("sect", "slab")),
        P(("sect", "slab")),
        P(("sect", "slab")),
        P(("sect", "slab")),
        P(("sect", "slab")),
        P(),
        P(),
        P(),
    )
    out_specs = (P(None, "slab", "sect"), P(None, ("sect", "slab")), P(None, ("sect", "slab")))
    return jax.shard_map(body, mesh=mesh, in_specs=in_specs, out_specs=out_specs, check_vma=False)
```

```python
import jax
import jax.numpy as jnp
from jax import lax
from jax.experimental import pallas as pl
from jax.experimental.pallas import tpu as pltpu
from jax.experimental.layout import Layout, with_layout_constraint
from jax.sharding import PartitionSpec as P

NC = 30
RR_ITERS = 4
MOVE_CAP = 1024
UNROLL = 8


def with_halo(block, sides, width):
    for axis, dim in sides:
        count = lax.axis_size(axis)
        forward = [(i, i + 1) for i in range(count - 1)]
        backward = [(target, source) for source, target in forward]
        low = lax.ppermute(
            lax.slice_in_dim(block, block.shape[dim] - width, None, axis=dim), axis, forward
        )
        high = lax.ppermute(lax.slice_in_dim(block, 0, width, axis=dim), axis, backward)
        block = jnp.concatenate([low, block, high], axis=dim)
    return block


def shifted(shard, axis, by):
    length = lax.axis_size(axis)
    pairs = [(i, i + by) for i in range(length) if 0 <= i + by < length]
    return lax.ppermute(shard, axis, pairs)


def parcel_update(masses, drop_temp, flags, vap_p, temp_p, volat_a, volat_b, latent):
    total = jnp.sum(masses, axis=0)
    frac = masses / total[None]
    surf = 0.5 * (drop_temp + temp_p)
    ratio = jnp.exp(volat_a[:, None] - volat_b[:, None] / surf[None])
    excess = ratio - 1.0
    share = jnp.full(total.shape, 0.5, jnp.float32)
    for sweep in range(RR_ITERS):
        denom = 1.0 + share[None] * excess
        residue = jnp.sum(frac * excess / denom, axis=0)
        slope = jnp.sum(frac * excess * excess / (denom * denom), axis=0) + 0.1
        share = jnp.clip(share + residue / slope, 0.02, 0.98)
    effect = flags.astype(jnp.float32) * share
    vap_eq = frac * ratio / (1.0 + effect[None] * excess)
    evap = 0.02 * total[None] * (vap_eq - vap_p)
    new_mass = masses - evap
    new_temp = (
        drop_temp
        + 0.2 * (temp_p - drop_temp)
        - 0.5 * jnp.sum(latent[:, None] * evap, axis=0) / total
    )
    heat = total * (drop_temp - temp_p)
    state = jnp.concatenate([new_mass, new_temp[None]], axis=0)
    terms = jnp.concatenate([0.1 * evap, 0.05 * heat[None]], axis=0)
    return (state, terms)


def pack_slots(state, chosen):
    slot = jnp.where(chosen, jnp.cumsum(chosen.astype(jnp.int32)) - 1, -1)
    onehot = (slot[:, None] == jnp.arange(MOVE_CAP, dtype=jnp.int32)[None, :]).astype(jnp.bfloat16)
    high = lax.reduce_precision(state, exponent_bits=8, mantissa_bits=7)
    rest = state - high
    middle = lax.reduce_precision(rest, exponent_bits=8, mantissa_bits=7)
    low = rest - middle
    parts = jnp.concatenate([high, middle, low], axis=0).astype(jnp.bfloat16)
    out = jnp.dot(parts, onehot, preferred_element_type=jnp.float32)
    rows = state.shape[0]
    return (out[:rows] + out[rows : 2 * rows]) + out[2 * rows :]


def _gather_kernel(count_ref, dst_ref, src_ref, table_ref, out_ref):
    out_ref[...] = jnp.zeros(out_ref.shape, out_ref.dtype)

    def step(i, carry):
        base = i * UNROLL
        for j in range(UNROLL):
            out_ref[pl.ds(dst_ref[base + j], 1), :] = table_ref[pl.ds(src_ref[base + j], 1), :]
        return carry

    lax.fori_loop(0, (count_ref[0] + UNROLL - 1) // UNROLL, step, 0)


def _scatter_kernel(count_ref, src_ref, seg_ref, rows_ref, out_ref, even_ref, odd_ref):
    even_ref[...] = jnp.zeros(even_ref.shape, even_ref.dtype)
    odd_ref[...] = jnp.zeros(odd_ref.shape, odd_ref.dtype)

    def step(i, carry):
        base = i * UNROLL
        for j in range(UNROLL):
            acc = even_ref if j % 2 == 0 else odd_ref
            acc[pl.ds(seg_ref[base + j], 1), :] += rows_ref[pl.ds(src_ref[base + j], 1), :]
        return carry

    lax.fori_loop(0, (count_ref[0] + UNROLL - 1) // UNROLL, step, 0)
    rows = out_ref.shape[0]
    out_ref[...] = even_ref[pl.ds(0, rows), :] + odd_ref[pl.ds(0, rows), :]


def row_gather(count, order, local, table):
    n_out = order.shape[0]
    n_tab, width = table.shape
    spec = pltpu.PrefetchScalarGridSpec(
        num_scalar_prefetch=3,
        grid=(1,),
        in_specs=[pl.BlockSpec((n_tab, width), lambda i, *_: (0, 0))],
        out_specs=pl.BlockSpec((n_out, width), lambda i, *_: (0, 0)),
    )
    return pl.pallas_call(
        _gather_kernel,
        grid_spec=spec,
        out_shape=jax.ShapeDtypeStruct((n_out, width), table.dtype),
    )(count, order, local, table)


def row_scatter_add(count, order, seg, rows, n_cells):
    n_rows, width = rows.shape
    spec = pltpu.PrefetchScalarGridSpec(
        num_scalar_prefetch=3,
        grid=(1,),
        in_specs=[pl.BlockSpec((n_rows, width), lambda i, *_: (0, 0))],
        out_specs=pl.BlockSpec((n_cells, width), lambda i, *_: (0, 0)),
        scratch_shapes=[pltpu.VMEM((n_cells + UNROLL, width), jnp.float32)] * 2,
    )
    return pl.pallas_call(
        _scatter_kernel,
        grid_spec=spec,
        out_shape=jax.ShapeDtypeStruct((n_cells, width), rows.dtype),
    )(count, order, seg, rows)


def field_major(x):
    return with_layout_constraint(x, Layout(major_to_minor=(0, 1)))


def body(vapor, gas_temp, masses, drop_temp, cells, flags, moves, volat_a, volat_b, latent):
    gas_block = jnp.concatenate([vapor, gas_temp[None]], axis=0)
    fields, width_x, width_yz = gas_block.shape
    n_cells = width_x * width_yz
    sections = lax.axis_size("sect")
    own_sect = lax.axis_index("sect")
    plane = sections * width_yz
    parcel_in = jnp.concatenate(
        [masses, drop_temp[None], flags.astype(jnp.float32)[None]], axis=0
    )
    all_in = field_major(lax.all_gather(field_major(parcel_in), "sect", axis=1, tiled=True))
    all_cells = lax.all_gather(cells.astype(jnp.float32), "sect", axis=0, tiled=True)
    all_cells = all_cells.astype(jnp.int32)
    n_all = all_cells.shape[0]
    cell_row = all_cells // plane
    cell_col = all_cells % plane
    owned = (cell_col // width_yz) == own_sect
    local_cell = (cell_row * width_yz + cell_col % width_yz).astype(jnp.int32)
    seg = jnp.where(owned, local_cell, n_cells).astype(jnp.int32)
    position = jnp.arange(n_all, dtype=jnp.int32)
    keys = jnp.where(owned, 0, n_all).astype(jnp.int32) + position
    _, order, local_sorted, seg_sorted = lax.sort(
        (keys, position, local_cell, seg), num_keys=1
    )
    count = jnp.sum(owned.astype(jnp.int32)).reshape(1)
    table = gas_block.reshape(fields, n_cells).T
    at_parcel = jnp.where(
        owned[None, :], row_gather(count, order, local_sorted, table).T, 0.0
    )
    state_all, terms_all = parcel_update(
        all_in[:NC], all_in[NC], all_in[NC + 1], at_parcel[:NC], at_parcel[NC],
        volat_a, volat_b, latent,
    )
    state_own = field_major(jnp.where(owned[None, :], state_all, 0.0))
    state = field_major(lax.psum_scatter(state_own, "sect", scatter_dimension=1, tiled=True))
    padded = with_halo(gas_block, (("slab", 1),), 1)
    down = padded[:, :-2]
    upper = padded[:, 2:]
    flowed = gas_block + 0.2 * (upper - 2.0 * gas_block + down) - 0.3 * (gas_block - down)
    summed = row_scatter_add(count, order, seg_sorted, terms_all.T, n_cells)
    source = summed.T.reshape(fields, width_x, width_yz)
    gas_next = flowed + source
    kept = jnp.where(moves[None] == 0, state, 0.0)
    from_prev = shifted(pack_slots(state, moves == 2), "slab", 1)
    from_next = shifted(pack_slots(state, moves == 1), "slab", -1)
    arrivals = jnp.concatenate([from_prev, from_next], axis=1)
    return (gas_next, kept, arrivals)


def solution(mesh):
    in_specs = (
        P(None, "slab", "sect"),
        P("slab", "sect"),
        P(None, ("sect", "slab")),
        P(("sect", "slab")),
        P(("sect", "slab")),
        P(("sect", "slab")),
        P(("sect", "slab")),
        P(),
        P(),
        P(),
    )
    out_specs = (P(None, "slab", "sect"), P(None, ("sect", "slab")), P(None, ("sect", "slab")))
    return jax.shard_map(body, mesh=mesh, in_specs=in_specs, out_specs=out_specs, check_vma=False)
```

```python
import jax
import jax.numpy as jnp
from jax import lax
from jax.experimental import pallas as pl
from jax.experimental.pallas import tpu as pltpu
from jax.experimental.layout import Layout, with_layout_constraint
from jax.sharding import PartitionSpec as P

NC = 30
RR_ITERS = 4
MOVE_CAP = 1024
UNROLL = 8


def with_halo(block, sides, width):
    for axis, dim in sides:
        count = lax.axis_size(axis)
        forward = [(i, i + 1) for i in range(count - 1)]
        backward = [(target, source) for source, target in forward]
        low = lax.ppermute(
            lax.slice_in_dim(block, block.shape[dim] - width, None, axis=dim), axis, forward
        )
        high = lax.ppermute(lax.slice_in_dim(block, 0, width, axis=dim), axis, backward)
        block = jnp.concatenate([low, block, high], axis=dim)
    return block


def shifted(shard, axis, by):
    length = lax.axis_size(axis)
    pairs = [(i, i + by) for i in range(length) if 0 <= i + by < length]
    return lax.ppermute(shard, axis, pairs)


def parcel_update(masses, drop_temp, flags, vap_p, temp_p, volat_a, volat_b, latent):
    total = jnp.sum(masses, axis=0)
    frac = masses / total[None]
    surf = 0.5 * (drop_temp + temp_p)
    ratio = jnp.exp(volat_a[:, None] - volat_b[:, None] / surf[None])
    excess = ratio - 1.0
    share = jnp.full(total.shape, 0.5, jnp.float32)
    for sweep in range(RR_ITERS):
        denom = 1.0 + share[None] * excess
        residue = jnp.sum(frac * excess / denom, axis=0)
        slope = jnp.sum(frac * excess * excess / (denom * denom), axis=0) + 0.1
        share = jnp.clip(share + residue / slope, 0.02, 0.98)
    effect = flags.astype(jnp.float32) * share
    vap_eq = frac * ratio / (1.0 + effect[None] * excess)
    evap = 0.02 * total[None] * (vap_eq - vap_p)
    new_mass = masses - evap
    new_temp = (
        drop_temp
        + 0.2 * (temp_p - drop_temp)
        - 0.5 * jnp.sum(latent[:, None] * evap, axis=0) / total
    )
    heat = total * (drop_temp - temp_p)
    state = jnp.concatenate([new_mass, new_temp[None]], axis=0)
    terms = jnp.concatenate([0.1 * evap, 0.05 * heat[None]], axis=0)
    return (state, terms)


def pack_slots(state, chosen):
    slot = jnp.where(chosen, jnp.cumsum(chosen.astype(jnp.int32)) - 1, -1)
    onehot = (slot[:, None] == jnp.arange(MOVE_CAP, dtype=jnp.int32)[None, :]).astype(jnp.bfloat16)
    high = lax.reduce_precision(state, exponent_bits=8, mantissa_bits=7)
    rest = state - high
    middle = lax.reduce_precision(rest, exponent_bits=8, mantissa_bits=7)
    low = rest - middle
    parts = jnp.concatenate([high, middle, low], axis=0).astype(jnp.bfloat16)
    out = jnp.dot(parts, onehot, preferred_element_type=jnp.float32)
    rows = state.shape[0]
    return (out[:rows] + out[rows : 2 * rows]) + out[2 * rows :]


def _gather_kernel(count_ref, dst_ref, src_ref, table_ref, out_ref):
    out_ref[...] = jnp.zeros(out_ref.shape, out_ref.dtype)

    def step(i, carry):
        base = i * UNROLL
        for j in range(UNROLL):
            out_ref[pl.ds(dst_ref[base + j], 1), :] = table_ref[pl.ds(src_ref[base + j], 1), :]
        return carry

    lax.fori_loop(0, (count_ref[0] + UNROLL - 1) // UNROLL, step, 0)


def _scatter_kernel(count_ref, src_ref, seg_ref, rows_ref, out_ref, even_ref, odd_ref):
    even_ref[...] = jnp.zeros(even_ref.shape, even_ref.dtype)
    odd_ref[...] = jnp.zeros(odd_ref.shape, odd_ref.dtype)

    def step(i, carry):
        base = i * UNROLL
        for j in range(UNROLL):
            acc = even_ref if j % 2 == 0 else odd_ref
            acc[pl.ds(seg_ref[base + j], 1), :] += rows_ref[pl.ds(src_ref[base + j], 1), :]
        return carry

    lax.fori_loop(0, (count_ref[0] + UNROLL - 1) // UNROLL, step, 0)
    rows = out_ref.shape[0]
    out_ref[...] = even_ref[pl.ds(0, rows), :] + odd_ref[pl.ds(0, rows), :]


def row_gather(count, order, local, table):
    n_out = order.shape[0]
    n_tab, width = table.shape
    spec = pltpu.PrefetchScalarGridSpec(
        num_scalar_prefetch=3,
        grid=(1,),
        in_specs=[pl.BlockSpec((n_tab, width), lambda i, *_: (0, 0))],
        out_specs=pl.BlockSpec((n_out, width), lambda i, *_: (0, 0)),
    )
    return pl.pallas_call(
        _gather_kernel,
        grid_spec=spec,
        out_shape=jax.ShapeDtypeStruct((n_out, width), table.dtype),
    )(count, order, local, table)


def row_scatter_add(count, order, seg, rows, n_cells):
    n_rows, width = rows.shape
    spec = pltpu.PrefetchScalarGridSpec(
        num_scalar_prefetch=3,
        grid=(1,),
        in_specs=[pl.BlockSpec((n_rows, width), lambda i, *_: (0, 0))],
        out_specs=pl.BlockSpec((n_cells, width), lambda i, *_: (0, 0)),
        scratch_shapes=[pltpu.VMEM((n_cells + UNROLL, width), jnp.float32)] * 2,
    )
    return pl.pallas_call(
        _scatter_kernel,
        grid_spec=spec,
        out_shape=jax.ShapeDtypeStruct((n_cells, width), rows.dtype),
    )(count, order, seg, rows)


def gather_sect(x):
    count = lax.axis_size("sect")
    own = lax.axis_index("sect")
    parts = [x] + [
        lax.ppermute(x, "sect", [(i, (i + k) % count) for i in range(count)])
        for k in range(1, count)
    ]
    stacked = jnp.stack(parts)
    where = (own - jnp.arange(count, dtype=jnp.int32)) % count
    return jnp.take(stacked, where, axis=0).reshape(-1)


def field_major(x):
    return with_layout_constraint(x, Layout(major_to_minor=(0, 1)))


def body(vapor, gas_temp, masses, drop_temp, cells, flags, moves, volat_a, volat_b, latent):
    gas_block = jnp.concatenate([vapor, gas_temp[None]], axis=0)
    fields, width_x, width_yz = gas_block.shape
    n_cells = width_x * width_yz
    sections = lax.axis_size("sect")
    own_sect = lax.axis_index("sect")
    plane = sections * width_yz
    parcel_in = jnp.concatenate(
        [masses, drop_temp[None], flags.astype(jnp.float32)[None]], axis=0
    )
    all_in = field_major(lax.all_gather(field_major(parcel_in), "sect", axis=1, tiled=True))
    all_cells = gather_sect(cells)
    n_all = all_cells.shape[0]
    cell_row = all_cells // plane
    cell_col = all_cells % plane
    owned = (cell_col // width_yz) == own_sect
    local_cell = (cell_row * width_yz + cell_col % width_yz).astype(jnp.int32)
    seg = jnp.where(owned, local_cell, n_cells).astype(jnp.int32)
    position = jnp.arange(n_all, dtype=jnp.int32)
    keys = jnp.where(owned, 0, n_all).astype(jnp.int32) + position
    _, order, local_sorted, seg_sorted = lax.sort(
        (keys, position, local_cell, seg), num_keys=1
    )
    count = jnp.sum(owned.astype(jnp.int32)).reshape(1)
    table = gas_block.reshape(fields, n_cells).T
    at_parcel = jnp.where(
        owned[None, :], row_gather(count, order, local_sorted, table).T, 0.0
    )
    state_all, terms_all = parcel_update(
        all_in[:NC], all_in[NC], all_in[NC + 1], at_parcel[:NC], at_parcel[NC],
        volat_a, volat_b, latent,
    )
    state_own = field_major(jnp.where(owned[None, :], state_all, 0.0))
    state = field_major(lax.psum_scatter(state_own, "sect", scatter_dimension=1, tiled=True))
    padded = with_halo(gas_block, (("slab", 1),), 1)
    down = padded[:, :-2]
    upper = padded[:, 2:]
    flowed = gas_block + 0.2 * (upper - 2.0 * gas_block + down) - 0.3 * (gas_block - down)
    summed = row_scatter_add(count, order, seg_sorted, terms_all.T, n_cells)
    source = summed.T.reshape(fields, width_x, width_yz)
    gas_next = flowed + source
    kept = jnp.where(moves[None] == 0, state, 0.0)
    from_prev = shifted(pack_slots(state, moves == 2), "slab", 1)
    from_next = shifted(pack_slots(state, moves == 1), "slab", -1)
    arrivals = jnp.concatenate([from_prev, from_next], axis=1)
    return (gas_next, kept, arrivals)


def solution(mesh):
    in_specs = (
        P(None, "slab", "sect"),
        P("slab", "sect"),
        P(None, ("sect", "slab")),
        P(("sect", "slab")),
        P(("sect", "slab")),
        P(("sect", "slab")),
        P(("sect", "slab")),
        P(),
        P(),
        P(),
    )
    out_specs = (P(None, "slab", "sect"), P(None, ("sect", "slab")), P(None, ("sect", "slab")))
    return jax.shard_map(body, mesh=mesh, in_specs=in_specs, out_specs=out_specs, check_vma=False)
```

```python
import jax
import jax.numpy as jnp
from jax import lax
from jax.experimental import pallas as pl
from jax.experimental.pallas import tpu as pltpu
from jax.experimental.layout import Layout, with_layout_constraint
from jax.sharding import PartitionSpec as P

NC = 30
RR_ITERS = 4
MOVE_CAP = 1024
UNROLL = 8


def with_halo(block, sides, width):
    for axis, dim in sides:
        count = lax.axis_size(axis)
        forward = [(i, i + 1) for i in range(count - 1)]
        backward = [(target, source) for source, target in forward]
        low = lax.ppermute(
            lax.slice_in_dim(block, block.shape[dim] - width, None, axis=dim), axis, forward
        )
        high = lax.ppermute(lax.slice_in_dim(block, 0, width, axis=dim), axis, backward)
        block = jnp.concatenate([low, block, high], axis=dim)
    return block


def shifted(shard, axis, by):
    length = lax.axis_size(axis)
    pairs = [(i, i + by) for i in range(length) if 0 <= i + by < length]
    return lax.ppermute(shard, axis, pairs)


def parcel_update(masses, drop_temp, flags, vap_p, temp_p, volat_a, volat_b, latent):
    total = jnp.sum(masses, axis=0)
    frac = masses / total[None]
    surf = 0.5 * (drop_temp + temp_p)
    ratio = jnp.exp(volat_a[:, None] - volat_b[:, None] / surf[None])
    excess = ratio - 1.0
    share = jnp.full(total.shape, 0.5, jnp.float32)
    for sweep in range(RR_ITERS):
        denom = 1.0 + share[None] * excess
        residue = jnp.sum(frac * excess / denom, axis=0)
        slope = jnp.sum(frac * excess * excess / (denom * denom), axis=0) + 0.1
        share = jnp.clip(share + residue / slope, 0.02, 0.98)
    effect = flags.astype(jnp.float32) * share
    vap_eq = frac * ratio / (1.0 + effect[None] * excess)
    evap = 0.02 * total[None] * (vap_eq - vap_p)
    new_mass = masses - evap
    new_temp = (
        drop_temp
        + 0.2 * (temp_p - drop_temp)
        - 0.5 * jnp.sum(latent[:, None] * evap, axis=0) / total
    )
    heat = total * (drop_temp - temp_p)
    state = jnp.concatenate([new_mass, new_temp[None]], axis=0)
    terms = jnp.concatenate([0.1 * evap, 0.05 * heat[None]], axis=0)
    return (state, terms)


def pack_slots(state, chosen):
    slot = jnp.where(chosen, jnp.cumsum(chosen.astype(jnp.int32)) - 1, -1)
    onehot = (slot[:, None] == jnp.arange(MOVE_CAP, dtype=jnp.int32)[None, :]).astype(jnp.bfloat16)
    high = lax.reduce_precision(state, exponent_bits=8, mantissa_bits=7)
    rest = state - high
    middle = lax.reduce_precision(rest, exponent_bits=8, mantissa_bits=7)
    low = rest - middle
    parts = jnp.concatenate([high, middle, low], axis=0).astype(jnp.bfloat16)
    out = jnp.dot(parts, onehot, preferred_element_type=jnp.float32)
    rows = state.shape[0]
    return (out[:rows] + out[rows : 2 * rows]) + out[2 * rows :]


def _gather_kernel(count_ref, dst_ref, src_ref, table_ref, out_ref):
    def step(i, carry):
        base = i * UNROLL
        for j in range(UNROLL):
            out_ref[pl.ds(dst_ref[base + j], 1), :] = table_ref[pl.ds(src_ref[base + j], 1), :]
        return carry

    lax.fori_loop(0, (count_ref[0] + UNROLL - 1) // UNROLL, step, 0)


def _scatter_kernel(count_ref, src_ref, seg_ref, rows_ref, out_ref, odd_ref):
    out_ref[...] = jnp.zeros(out_ref.shape, out_ref.dtype)
    odd_ref[...] = jnp.zeros(odd_ref.shape, odd_ref.dtype)

    def add_row(acc, k):
        acc[pl.ds(seg_ref[k], 1), :] += rows_ref[pl.ds(src_ref[k], 1), :]

    def step(i, carry):
        base = i * UNROLL
        for j in range(UNROLL):
            add_row(out_ref if j % 2 == 0 else odd_ref, base + j)
        return carry

    def rest(k, carry):
        add_row(out_ref, k)
        return carry

    full = count_ref[0] // UNROLL
    lax.fori_loop(0, full, step, 0)
    lax.fori_loop(full * UNROLL, count_ref[0], rest, 0)
    out_ref[...] += odd_ref[...]


def row_gather(count, order, local, table):
    n_out = order.shape[0]
    n_tab, width = table.shape
    spec = pltpu.PrefetchScalarGridSpec(
        num_scalar_prefetch=3,
        grid=(1,),
        in_specs=[pl.BlockSpec((n_tab, width), lambda i, *_: (0, 0))],
        out_specs=pl.BlockSpec((n_out, width), lambda i, *_: (0, 0)),
    )
    return pl.pallas_call(
        _gather_kernel,
        grid_spec=spec,
        out_shape=jax.ShapeDtypeStruct((n_out, width), table.dtype),
    )(count, order, local, table)


def row_scatter_add(count, order, seg, rows, n_cells):
    n_rows, width = rows.shape
    spec = pltpu.PrefetchScalarGridSpec(
        num_scalar_prefetch=3,
        grid=(1,),
        in_specs=[pl.BlockSpec((n_rows, width), lambda i, *_: (0, 0))],
        out_specs=pl.BlockSpec((n_cells, width), lambda i, *_: (0, 0)),
        scratch_shapes=[pltpu.VMEM((n_cells, width), jnp.float32)],
    )
    return pl.pallas_call(
        _scatter_kernel,
        grid_spec=spec,
        out_shape=jax.ShapeDtypeStruct((n_cells, width), rows.dtype),
    )(count, order, seg, rows)


def gather_sect(x):
    count = lax.axis_size("sect")
    own = lax.axis_index("sect")
    parts = [x] + [
        lax.ppermute(x, "sect", [(i, (i + k) % count) for i in range(count)])
        for k in range(1, count)
    ]
    stacked = jnp.stack(parts)
    where = (own - jnp.arange(count, dtype=jnp.int32)) % count
    return jnp.take(stacked, where, axis=0).reshape(-1)


def field_major(x):
    return with_layout_constraint(x, Layout(major_to_minor=(0, 1)))


def body(vapor, gas_temp, masses, drop_temp, cells, flags, moves, volat_a, volat_b, latent):
    gas_block = jnp.concatenate([vapor, gas_temp[None]], axis=0)
    fields, width_x, width_yz = gas_block.shape
    n_cells = width_x * width_yz
    sections = lax.axis_size("sect")
    own_sect = lax.axis_index("sect")
    plane = sections * width_yz
    parcel_in = jnp.concatenate(
        [masses, drop_temp[None], flags.astype(jnp.float32)[None]], axis=0
    )
    all_in = field_major(lax.all_gather(field_major(parcel_in), "sect", axis=1, tiled=True))
    all_cells = gather_sect(cells)
    n_all = all_cells.shape[0]
    cell_row = all_cells // plane
    cell_col = all_cells % plane
    owned = (cell_col // width_yz) == own_sect
    local_cell = (cell_row * width_yz + cell_col % width_yz).astype(jnp.int32)
    seg = jnp.where(owned, local_cell, n_cells).astype(jnp.int32)
    position = jnp.arange(n_all, dtype=jnp.int32)
    keys = jnp.where(owned, 0, n_all).astype(jnp.int32) + position
    _, order, local_sorted, seg_sorted = lax.sort(
        (keys, position, local_cell, seg), num_keys=1
    )
    count = jnp.sum(owned.astype(jnp.int32)).reshape(1)
    table = gas_block.reshape(fields, n_cells).T
    at_parcel = jnp.where(
        owned[None, :], row_gather(count, order, local_sorted, table).T, 0.0
    )
    state_all, terms_all = parcel_update(
        all_in[:NC], all_in[NC], all_in[NC + 1], at_parcel[:NC], at_parcel[NC],
        volat_a, volat_b, latent,
    )
    state_own = field_major(jnp.where(owned[None, :], state_all, 0.0))
    state = field_major(lax.psum_scatter(state_own, "sect", scatter_dimension=1, tiled=True))
    padded = with_halo(gas_block, (("slab", 1),), 1)
    down = padded[:, :-2]
    upper = padded[:, 2:]
    flowed = gas_block + 0.2 * (upper - 2.0 * gas_block + down) - 0.3 * (gas_block - down)
    summed = row_scatter_add(count, order, seg_sorted, terms_all.T, n_cells)
    source = summed.T.reshape(fields, width_x, width_yz)
    gas_next = flowed + source
    kept = jnp.where(moves[None] == 0, state, 0.0)
    from_prev = shifted(pack_slots(state, moves == 2), "slab", 1)
    from_next = shifted(pack_slots(state, moves == 1), "slab", -1)
    arrivals = jnp.concatenate([from_prev, from_next], axis=1)
    return (gas_next, kept, arrivals)


def solution(mesh):
    in_specs = (
        P(None, "slab", "sect"),
        P("slab", "sect"),
        P(None, ("sect", "slab")),
        P(("sect", "slab")),
        P(("sect", "slab")),
        P(("sect", "slab")),
        P(("sect", "slab")),
        P(),
        P(),
        P(),
    )
    out_specs = (P(None, "slab", "sect"), P(None, ("sect", "slab")), P(None, ("sect", "slab")))
    return jax.shard_map(body, mesh=mesh, in_specs=in_specs, out_specs=out_specs, check_vma=False)
```

```python
import jax
import jax.numpy as jnp
from jax import lax
from jax.experimental import pallas as pl
from jax.experimental.pallas import tpu as pltpu
from jax.experimental.layout import Layout, with_layout_constraint
from jax.sharding import PartitionSpec as P

NC = 30
RR_ITERS = 4
MOVE_CAP = 1024
UNROLL = 8


def with_halo(block, sides, width):
    for axis, dim in sides:
        count = lax.axis_size(axis)
        forward = [(i, i + 1) for i in range(count - 1)]
        backward = [(target, source) for source, target in forward]
        low = lax.ppermute(
            lax.slice_in_dim(block, block.shape[dim] - width, None, axis=dim), axis, forward
        )
        high = lax.ppermute(lax.slice_in_dim(block, 0, width, axis=dim), axis, backward)
        block = jnp.concatenate([low, block, high], axis=dim)
    return block


def shifted(shard, axis, by):
    length = lax.axis_size(axis)
    pairs = [(i, i + by) for i in range(length) if 0 <= i + by < length]
    return lax.ppermute(shard, axis, pairs)


def parcel_update(masses, drop_temp, flags, vap_p, temp_p, volat_a, volat_b, latent):
    total = jnp.sum(masses, axis=0)
    frac = masses / total[None]
    surf = 0.5 * (drop_temp + temp_p)
    ratio = jnp.exp(volat_a[:, None] - volat_b[:, None] / surf[None])
    excess = ratio - 1.0
    share = jnp.full(total.shape, 0.5, jnp.float32)
    for sweep in range(RR_ITERS):
        denom = 1.0 + share[None] * excess
        residue = jnp.sum(frac * excess / denom, axis=0)
        slope = jnp.sum(frac * excess * excess / (denom * denom), axis=0) + 0.1
        share = jnp.clip(share + residue / slope, 0.02, 0.98)
    effect = flags.astype(jnp.float32) * share
    vap_eq = frac * ratio / (1.0 + effect[None] * excess)
    evap = 0.02 * total[None] * (vap_eq - vap_p)
    new_mass = masses - evap
    new_temp = (
        drop_temp
        + 0.2 * (temp_p - drop_temp)
        - 0.5 * jnp.sum(latent[:, None] * evap, axis=0) / total
    )
    heat = total * (drop_temp - temp_p)
    state = jnp.concatenate([new_mass, new_temp[None]], axis=0)
    terms = jnp.concatenate([0.1 * evap, 0.05 * heat[None]], axis=0)
    return (state, terms)


def pack_slots(state, chosen):
    slot = jnp.where(chosen, jnp.cumsum(chosen.astype(jnp.int32)) - 1, -1)
    onehot = (slot[:, None] == jnp.arange(MOVE_CAP, dtype=jnp.int32)[None, :]).astype(jnp.bfloat16)
    high = lax.reduce_precision(state, exponent_bits=8, mantissa_bits=7)
    rest = state - high
    middle = lax.reduce_precision(rest, exponent_bits=8, mantissa_bits=7)
    low = rest - middle
    parts = jnp.concatenate([high, middle, low], axis=0).astype(jnp.bfloat16)
    out = jnp.dot(parts, onehot, preferred_element_type=jnp.float32)
    rows = state.shape[0]
    return (out[:rows] + out[rows : 2 * rows]) + out[2 * rows :]


def _gather_kernel(count_ref, dst_ref, src_ref, table_ref, out_ref):
    def step(i, carry):
        base = i * UNROLL
        for j in range(UNROLL):
            out_ref[pl.ds(dst_ref[base + j], 1), :] = table_ref[pl.ds(src_ref[base + j], 1), :]
        return carry

    lax.fori_loop(0, (count_ref[0] + UNROLL - 1) // UNROLL, step, 0)


def _scatter_kernel(count_ref, src_ref, seg_ref, rows_ref, out_ref, odd_ref):
    out_ref[...] = jnp.zeros(out_ref.shape, out_ref.dtype)
    odd_ref[...] = jnp.zeros(odd_ref.shape, odd_ref.dtype)

    def add_row(acc, k):
        acc[pl.ds(seg_ref[k], 1), :] += rows_ref[pl.ds(src_ref[k], 1), :]

    def step(i, carry):
        base = i * UNROLL
        for j in range(UNROLL):
            add_row(out_ref if j % 2 == 0 else odd_ref, base + j)
        return carry

    def rest(k, carry):
        add_row(out_ref, k)
        return carry

    full = count_ref[0] // UNROLL
    lax.fori_loop(0, full, step, 0)
    lax.fori_loop(full * UNROLL, count_ref[0], rest, 0)
    out_ref[...] += odd_ref[...]


def row_gather(count, order, local, table):
    n_out = order.shape[0]
    n_tab, width = table.shape
    spec = pltpu.PrefetchScalarGridSpec(
        num_scalar_prefetch=3,
        grid=(1,),
        in_specs=[pl.BlockSpec((n_tab, width), lambda i, *_: (0, 0))],
        out_specs=pl.BlockSpec((n_out, width), lambda i, *_: (0, 0)),
    )
    return pl.pallas_call(
        _gather_kernel,
        grid_spec=spec,
        out_shape=jax.ShapeDtypeStruct((n_out, width), table.dtype),
    )(count, order, local, table)


def row_scatter_add(count, order, seg, rows, n_cells):
    n_rows, width = rows.shape
    spec = pltpu.PrefetchScalarGridSpec(
        num_scalar_prefetch=3,
        grid=(1,),
        in_specs=[pl.BlockSpec((n_rows, width), lambda i, *_: (0, 0))],
        out_specs=pl.BlockSpec((n_cells, width), lambda i, *_: (0, 0)),
        scratch_shapes=[pltpu.VMEM((n_cells, width), jnp.float32)],
    )
    return pl.pallas_call(
        _scatter_kernel,
        grid_spec=spec,
        out_shape=jax.ShapeDtypeStruct((n_cells, width), rows.dtype),
    )(count, order, seg, rows)


def gather_sect(x):
    count = lax.axis_size("sect")
    own = lax.axis_index("sect")
    parts = [x] + [
        lax.ppermute(x, "sect", [(i, (i + k) % count) for i in range(count)])
        for k in range(1, count)
    ]
    stacked = jnp.stack(parts)
    where = (own - jnp.arange(count, dtype=jnp.int32)) % count
    return jnp.take(stacked, where, axis=0).reshape(-1)


def field_major(x):
    return with_layout_constraint(x, Layout(major_to_minor=(0, 1)))


def plane_major(x):
    return with_layout_constraint(x, Layout(major_to_minor=(0, 1, 2)))


def body(vapor, gas_temp, masses, drop_temp, cells, flags, moves, volat_a, volat_b, latent):
    gas_block = jnp.concatenate([vapor, gas_temp[None]], axis=0)
    fields, width_x, width_yz = gas_block.shape
    n_cells = width_x * width_yz
    sections = lax.axis_size("sect")
    own_sect = lax.axis_index("sect")
    plane = sections * width_yz
    parcel_in = jnp.concatenate(
        [masses, drop_temp[None], flags.astype(jnp.float32)[None]], axis=0
    )
    all_in = field_major(lax.all_gather(field_major(parcel_in), "sect", axis=1, tiled=True))
    all_cells = gather_sect(cells)
    n_all = all_cells.shape[0]
    cell_row = all_cells // plane
    cell_col = all_cells % plane
    owned = (cell_col // width_yz) == own_sect
    local_cell = (cell_row * width_yz + cell_col % width_yz).astype(jnp.int32)
    seg = jnp.where(owned, local_cell, n_cells).astype(jnp.int32)
    position = jnp.arange(n_all, dtype=jnp.int32)
    keys = jnp.where(owned, 0, n_all).astype(jnp.int32) + position
    _, order, local_sorted, seg_sorted = lax.sort(
        (keys, position, local_cell, seg), num_keys=1
    )
    count = jnp.sum(owned.astype(jnp.int32)).reshape(1)
    table = gas_block.reshape(fields, n_cells).T
    at_parcel = jnp.where(
        owned[None, :], row_gather(count, order, local_sorted, table).T, 0.0
    )
    state_all, terms_all = parcel_update(
        all_in[:NC], all_in[NC], all_in[NC + 1], at_parcel[:NC], at_parcel[NC],
        volat_a, volat_b, latent,
    )
    state_own = field_major(jnp.where(owned[None, :], state_all, 0.0))
    state = field_major(lax.psum_scatter(state_own, "sect", scatter_dimension=1, tiled=True))
    padded = with_halo(gas_block, (("slab", 1),), 1)
    down = padded[:, :-2]
    upper = padded[:, 2:]
    flowed = plane_major(
        gas_block + 0.2 * (upper - 2.0 * gas_block + down) - 0.3 * (gas_block - down)
    )
    summed = row_scatter_add(count, order, seg_sorted, terms_all.T, n_cells)
    source = plane_major(summed.T.reshape(fields, width_x, width_yz))
    gas_next = plane_major(flowed + source)
    kept = jnp.where(moves[None] == 0, state, 0.0)
    from_prev = shifted(pack_slots(state, moves == 2), "slab", 1)
    from_next = shifted(pack_slots(state, moves == 1), "slab", -1)
    arrivals = jnp.concatenate([from_prev, from_next], axis=1)
    return (gas_next, kept, arrivals)


def solution(mesh):
    in_specs = (
        P(None, "slab", "sect"),
        P("slab", "sect"),
        P(None, ("sect", "slab")),
        P(("sect", "slab")),
        P(("sect", "slab")),
        P(("sect", "slab")),
        P(("sect", "slab")),
        P(),
        P(),
        P(),
    )
    out_specs = (P(None, "slab", "sect"), P(None, ("sect", "slab")), P(None, ("sect", "slab")))
    return jax.shard_map(body, mesh=mesh, in_specs=in_specs, out_specs=out_specs, check_vma=False)
```

```python
import jax
import jax.numpy as jnp
from jax import lax
from jax.experimental import pallas as pl
from jax.experimental.pallas import tpu as pltpu
from jax.experimental.layout import Layout, with_layout_constraint
from jax.sharding import PartitionSpec as P

NC = 30
RR_ITERS = 4
MOVE_CAP = 1024
UNROLL = 8


def with_halo(block, sides, width):
    for axis, dim in sides:
        count = lax.axis_size(axis)
        forward = [(i, i + 1) for i in range(count - 1)]
        backward = [(target, source) for source, target in forward]
        low = lax.ppermute(
            lax.slice_in_dim(block, block.shape[dim] - width, None, axis=dim), axis, forward
        )
        high = lax.ppermute(lax.slice_in_dim(block, 0, width, axis=dim), axis, backward)
        block = jnp.concatenate([low, block, high], axis=dim)
    return block


def shifted(shard, axis, by):
    length = lax.axis_size(axis)
    pairs = [(i, i + by) for i in range(length) if 0 <= i + by < length]
    return lax.ppermute(shard, axis, pairs)


def parcel_update(masses, drop_temp, flags, vap_p, temp_p, volat_a, volat_b, latent):
    total = jnp.sum(masses, axis=0)
    frac = masses / total[None]
    surf = 0.5 * (drop_temp + temp_p)
    ratio = jnp.exp(volat_a[:, None] - volat_b[:, None] / surf[None])
    excess = ratio - 1.0
    share = jnp.full(total.shape, 0.5, jnp.float32)
    for sweep in range(RR_ITERS):
        denom = 1.0 + share[None] * excess
        residue = jnp.sum(frac * excess / denom, axis=0)
        slope = jnp.sum(frac * excess * excess / (denom * denom), axis=0) + 0.1
        share = jnp.clip(share + residue / slope, 0.02, 0.98)
    effect = flags.astype(jnp.float32) * share
    vap_eq = frac * ratio / (1.0 + effect[None] * excess)
    evap = 0.02 * total[None] * (vap_eq - vap_p)
    new_mass = masses - evap
    new_temp = (
        drop_temp
        + 0.2 * (temp_p - drop_temp)
        - 0.5 * jnp.sum(latent[:, None] * evap, axis=0) / total
    )
    heat = total * (drop_temp - temp_p)
    state = jnp.concatenate([new_mass, new_temp[None]], axis=0)
    terms = jnp.concatenate([0.1 * evap, 0.05 * heat[None]], axis=0)
    return (state, terms)


def pack_slots(state, chosen):
    slot = jnp.where(chosen, jnp.cumsum(chosen.astype(jnp.int32)) - 1, -1)
    onehot = (slot[:, None] == jnp.arange(MOVE_CAP, dtype=jnp.int32)[None, :]).astype(jnp.bfloat16)
    high = lax.reduce_precision(state, exponent_bits=8, mantissa_bits=7)
    rest = state - high
    middle = lax.reduce_precision(rest, exponent_bits=8, mantissa_bits=7)
    low = rest - middle
    parts = jnp.concatenate([high, middle, low], axis=0).astype(jnp.bfloat16)
    out = jnp.dot(parts, onehot, preferred_element_type=jnp.float32)
    rows = state.shape[0]
    return (out[:rows] + out[rows : 2 * rows]) + out[2 * rows :]


def _gather_kernel(count_ref, dst_ref, src_ref, table_ref, out_ref):
    def step(i, carry):
        base = i * UNROLL
        for j in range(UNROLL):
            out_ref[pl.ds(dst_ref[base + j], 1), :] = table_ref[pl.ds(src_ref[base + j], 1), :]
        return carry

    lax.fori_loop(0, (count_ref[0] + UNROLL - 1) // UNROLL, step, 0)


def _scatter_kernel(count_ref, src_ref, seg_ref, rows_ref, out_ref, odd_ref):
    out_ref[...] = jnp.zeros(out_ref.shape, out_ref.dtype)
    odd_ref[...] = jnp.zeros(odd_ref.shape, odd_ref.dtype)

    def add_row(acc, k):
        acc[pl.ds(seg_ref[k], 1), :] += rows_ref[pl.ds(src_ref[k], 1), :]

    def step(i, carry):
        base = i * UNROLL
        for j in range(UNROLL):
            add_row(out_ref if j % 2 == 0 else odd_ref, base + j)
        return carry

    def rest(k, carry):
        add_row(out_ref, k)
        return carry

    full = count_ref[0] // UNROLL
    lax.fori_loop(0, full, step, 0)
    lax.fori_loop(full * UNROLL, count_ref[0], rest, 0)
    out_ref[...] += odd_ref[...]


def row_gather(count, order, local, table):
    n_out = order.shape[0]
    n_tab, width = table.shape
    spec = pltpu.PrefetchScalarGridSpec(
        num_scalar_prefetch=3,
        grid=(1,),
        in_specs=[pl.BlockSpec((n_tab, width), lambda i, *_: (0, 0))],
        out_specs=pl.BlockSpec((n_out, width), lambda i, *_: (0, 0)),
    )
    return pl.pallas_call(
        _gather_kernel,
        grid_spec=spec,
        out_shape=jax.ShapeDtypeStruct((n_out, width), table.dtype),
    )(count, order, local, table)


def row_scatter_add(count, order, seg, rows, n_cells):
    n_rows, width = rows.shape
    spec = pltpu.PrefetchScalarGridSpec(
        num_scalar_prefetch=3,
        grid=(1,),
        in_specs=[pl.BlockSpec((n_rows, width), lambda i, *_: (0, 0))],
        out_specs=pl.BlockSpec((n_cells, width), lambda i, *_: (0, 0)),
        scratch_shapes=[pltpu.VMEM((n_cells, width), jnp.float32)],
    )
    return pl.pallas_call(
        _scatter_kernel,
        grid_spec=spec,
        out_shape=jax.ShapeDtypeStruct((n_cells, width), rows.dtype),
    )(count, order, seg, rows)


def gather_sect(x):
    count = lax.axis_size("sect")
    own = lax.axis_index("sect")
    parts = [x] + [
        lax.ppermute(x, "sect", [(i, (i + k) % count) for i in range(count)])
        for k in range(1, count)
    ]
    stacked = jnp.stack(parts)
    where = (own - jnp.arange(count, dtype=jnp.int32)) % count
    return jnp.take(stacked, where, axis=0).reshape(-1)


def field_major(x):
    return with_layout_constraint(x, Layout(major_to_minor=(0, 1)))


def plane_major(x):
    return with_layout_constraint(x, Layout(major_to_minor=(0, 1, 2)))


def body(vapor, gas_temp, masses, drop_temp, cells, flags, moves, volat_a, volat_b, latent):
    gas_block = jnp.concatenate([vapor, gas_temp[None]], axis=0)
    fields, width_x, width_yz = gas_block.shape
    n_cells = width_x * width_yz
    sections = lax.axis_size("sect")
    own_sect = lax.axis_index("sect")
    plane = sections * width_yz
    parcel_in = jnp.concatenate(
        [masses, drop_temp[None], flags.astype(jnp.float32)[None]], axis=0
    )
    all_in = plane_major(lax.all_gather(field_major(parcel_in), "sect", axis=0, tiled=False))
    all_cells = gather_sect(cells)
    n_all = all_cells.shape[0]
    cell_row = all_cells // plane
    cell_col = all_cells % plane
    owned = (cell_col // width_yz) == own_sect
    local_cell = (cell_row * width_yz + cell_col % width_yz).astype(jnp.int32)
    seg = jnp.where(owned, local_cell, n_cells).astype(jnp.int32)
    position = jnp.arange(n_all, dtype=jnp.int32)
    keys = jnp.where(owned, 0, n_all).astype(jnp.int32) + position
    _, order, local_sorted, seg_sorted = lax.sort(
        (keys, position, local_cell, seg), num_keys=1
    )
    count = jnp.sum(owned.astype(jnp.int32)).reshape(1)
    table = gas_block.reshape(fields, n_cells).T
    blocks = all_in.shape[0]
    owned_blocks = owned.reshape(blocks, 1, -1)
    gathered = row_gather(count, order, local_sorted, table)
    gathered = gathered.reshape(blocks, -1, fields).transpose(0, 2, 1)
    at_parcel = plane_major(jnp.where(owned_blocks, gathered, 0.0))
    state_all, terms_all = jax.vmap(
        parcel_update, in_axes=(0, 0, 0, 0, 0, None, None, None)
    )(
        all_in[:, :NC], all_in[:, NC], all_in[:, NC + 1], at_parcel[:, :NC], at_parcel[:, NC],
        volat_a, volat_b, latent,
    )
    state_own = plane_major(jnp.where(owned_blocks, state_all, 0.0))
    state = field_major(lax.psum_scatter(state_own, "sect", scatter_dimension=0, tiled=False))
    padded = with_halo(gas_block, (("slab", 1),), 1)
    down = padded[:, :-2]
    upper = padded[:, 2:]
    flowed = plane_major(
        gas_block + 0.2 * (upper - 2.0 * gas_block + down) - 0.3 * (gas_block - down)
    )
    terms_rows = terms_all.transpose(0, 2, 1).reshape(-1, fields)
    summed = row_scatter_add(count, order, seg_sorted, terms_rows, n_cells)
    source = plane_major(summed.T.reshape(fields, width_x, width_yz))
    gas_next = plane_major(flowed + source)
    kept = jnp.where(moves[None] == 0, state, 0.0)
    from_prev = shifted(pack_slots(state, moves == 2), "slab", 1)
    from_next = shifted(pack_slots(state, moves == 1), "slab", -1)
    arrivals = jnp.concatenate([from_prev, from_next], axis=1)
    return (gas_next, kept, arrivals)


def solution(mesh):
    in_specs = (
        P(None, "slab", "sect"),
        P("slab", "sect"),
        P(None, ("sect", "slab")),
        P(("sect", "slab")),
        P(("sect", "slab")),
        P(("sect", "slab")),
        P(("sect", "slab")),
        P(),
        P(),
        P(),
    )
    out_specs = (P(None, "slab", "sect"), P(None, ("sect", "slab")), P(None, ("sect", "slab")))
    return jax.shard_map(body, mesh=mesh, in_specs=in_specs, out_specs=out_specs, check_vma=False)
```

```python
import jax
import jax.numpy as jnp
from jax import lax
from jax.experimental import pallas as pl
from jax.experimental.pallas import tpu as pltpu
from jax.experimental.layout import Layout, with_layout_constraint
from jax.sharding import PartitionSpec as P

NC = 30
RR_ITERS = 4
MOVE_CAP = 1024
UNROLL = 8


def with_halo(block, sides, width):
    for axis, dim in sides:
        count = lax.axis_size(axis)
        forward = [(i, i + 1) for i in range(count - 1)]
        backward = [(target, source) for source, target in forward]
        low = lax.ppermute(
            lax.slice_in_dim(block, block.shape[dim] - width, None, axis=dim), axis, forward
        )
        high = lax.ppermute(lax.slice_in_dim(block, 0, width, axis=dim), axis, backward)
        block = jnp.concatenate([low, block, high], axis=dim)
    return block


def shifted(shard, axis, by):
    length = lax.axis_size(axis)
    pairs = [(i, i + by) for i in range(length) if 0 <= i + by < length]
    return lax.ppermute(shard, axis, pairs)


def parcel_update(masses, drop_temp, flags, vap_p, temp_p, volat_a, volat_b, latent):
    total = jnp.sum(masses, axis=0)
    inv_total = 1.0 / total
    frac = masses * inv_total[None]
    surf = 0.5 * (drop_temp + temp_p)
    ratio = jnp.exp(volat_a[:, None] - volat_b[:, None] / surf[None])
    excess = ratio - 1.0
    weighted = frac * excess
    share = jnp.full(total.shape, 0.5, jnp.float32)
    for sweep in range(RR_ITERS):
        inv_denom = 1.0 / (1.0 + share[None] * excess)
        part = weighted * inv_denom
        residue = jnp.sum(part, axis=0)
        slope = jnp.sum(part * excess * inv_denom, axis=0) + 0.1
        share = jnp.clip(share + residue / slope, 0.02, 0.98)
    effect = flags.astype(jnp.float32) * share
    vap_eq = frac * ratio / (1.0 + effect[None] * excess)
    evap = 0.02 * total[None] * (vap_eq - vap_p)
    new_mass = masses - evap
    new_temp = (
        drop_temp
        + 0.2 * (temp_p - drop_temp)
        - 0.5 * jnp.sum(latent[:, None] * evap, axis=0) * inv_total
    )
    heat = total * (drop_temp - temp_p)
    state = jnp.concatenate([new_mass, new_temp[None]], axis=0)
    terms = jnp.concatenate([0.1 * evap, 0.05 * heat[None]], axis=0)
    return (state, terms)


def pack_slots(state, chosen):
    slot = jnp.where(chosen, jnp.cumsum(chosen.astype(jnp.int32)) - 1, -1)
    onehot = (slot[:, None] == jnp.arange(MOVE_CAP, dtype=jnp.int32)[None, :]).astype(jnp.bfloat16)
    high = lax.reduce_precision(state, exponent_bits=8, mantissa_bits=7)
    rest = state - high
    middle = lax.reduce_precision(rest, exponent_bits=8, mantissa_bits=7)
    low = rest - middle
    parts = jnp.concatenate([high, middle, low], axis=0).astype(jnp.bfloat16)
    out = jnp.dot(parts, onehot, preferred_element_type=jnp.float32)
    rows = state.shape[0]
    return (out[:rows] + out[rows : 2 * rows]) + out[2 * rows :]


def _gather_kernel(count_ref, dst_ref, src_ref, table_ref, out_ref):
    def step(i, carry):
        base = i * UNROLL
        for j in range(UNROLL):
            out_ref[pl.ds(dst_ref[base + j], 1), :] = table_ref[pl.ds(src_ref[base + j], 1), :]
        return carry

    lax.fori_loop(0, (count_ref[0] + UNROLL - 1) // UNROLL, step, 0)


def _scatter_kernel(count_ref, src_ref, seg_ref, rows_ref, out_ref, odd_ref):
    out_ref[...] = jnp.zeros(out_ref.shape, out_ref.dtype)
    odd_ref[...] = jnp.zeros(odd_ref.shape, odd_ref.dtype)

    def add_row(acc, k):
        acc[pl.ds(seg_ref[k], 1), :] += rows_ref[pl.ds(src_ref[k], 1), :]

    def step(i, carry):
        base = i * UNROLL
        for j in range(UNROLL):
            add_row(out_ref if j % 2 == 0 else odd_ref, base + j)
        return carry

    def rest(k, carry):
        add_row(out_ref, k)
        return carry

    full = count_ref[0] // UNROLL
    lax.fori_loop(0, full, step, 0)
    lax.fori_loop(full * UNROLL, count_ref[0], rest, 0)
    out_ref[...] += odd_ref[...]


def row_gather(count, order, local, table):
    n_out = order.shape[0]
    n_tab, width = table.shape
    spec = pltpu.PrefetchScalarGridSpec(
        num_scalar_prefetch=3,
        grid=(1,),
        in_specs=[pl.BlockSpec((n_tab, width), lambda i, *_: (0, 0))],
        out_specs=pl.BlockSpec((n_out, width), lambda i, *_: (0, 0)),
    )
    return pl.pallas_call(
        _gather_kernel,
        grid_spec=spec,
        out_shape=jax.ShapeDtypeStruct((n_out, width), table.dtype),
    )(count, order, local, table)


def row_scatter_add(count, order, seg, rows, n_cells):
    n_rows, width = rows.shape
    spec = pltpu.PrefetchScalarGridSpec(
        num_scalar_prefetch=3,
        grid=(1,),
        in_specs=[pl.BlockSpec((n_rows, width), lambda i, *_: (0, 0))],
        out_specs=pl.BlockSpec((n_cells, width), lambda i, *_: (0, 0)),
        scratch_shapes=[pltpu.VMEM((n_cells, width), jnp.float32)],
    )
    return pl.pallas_call(
        _scatter_kernel,
        grid_spec=spec,
        out_shape=jax.ShapeDtypeStruct((n_cells, width), rows.dtype),
    )(count, order, seg, rows)


def gather_sect(x):
    count = lax.axis_size("sect")
    own = lax.axis_index("sect")
    parts = [x] + [
        lax.ppermute(x, "sect", [(i, (i + k) % count) for i in range(count)])
        for k in range(1, count)
    ]
    stacked = jnp.stack(parts)
    where = (own - jnp.arange(count, dtype=jnp.int32)) % count
    return jnp.take(stacked, where, axis=0).reshape(-1)


def field_major(x):
    return with_layout_constraint(x, Layout(major_to_minor=(0, 1)))


def plane_major(x):
    return with_layout_constraint(x, Layout(major_to_minor=(0, 1, 2)))


def body(vapor, gas_temp, masses, drop_temp, cells, flags, moves, volat_a, volat_b, latent):
    gas_block = jnp.concatenate([vapor, gas_temp[None]], axis=0)
    fields, width_x, width_yz = gas_block.shape
    n_cells = width_x * width_yz
    sections = lax.axis_size("sect")
    own_sect = lax.axis_index("sect")
    plane = sections * width_yz
    parcel_in = jnp.concatenate(
        [masses, drop_temp[None], flags.astype(jnp.float32)[None]], axis=0
    )
    all_in = plane_major(lax.all_gather(field_major(parcel_in), "sect", axis=0, tiled=False))
    all_cells = gather_sect(cells)
    n_all = all_cells.shape[0]
    cell_row = all_cells // plane
    cell_col = all_cells % plane
    owned = (cell_col // width_yz) == own_sect
    local_cell = (cell_row * width_yz + cell_col % width_yz).astype(jnp.int32)
    seg = jnp.where(owned, local_cell, n_cells).astype(jnp.int32)
    position = jnp.arange(n_all, dtype=jnp.int32)
    keys = jnp.where(owned, 0, n_all).astype(jnp.int32) + position
    _, order, local_sorted, seg_sorted = lax.sort(
        (keys, position, local_cell, seg), num_keys=1
    )
    count = jnp.sum(owned.astype(jnp.int32)).reshape(1)
    table = gas_block.reshape(fields, n_cells).T
    blocks = all_in.shape[0]
    owned_blocks = owned.reshape(blocks, 1, -1)
    gathered = row_gather(count, order, local_sorted, table)
    gathered = gathered.reshape(blocks, -1, fields).transpose(0, 2, 1)
    at_parcel = plane_major(jnp.where(owned_blocks, gathered, 0.0))
    state_all, terms_all = jax.vmap(
        parcel_update, in_axes=(0, 0, 0, 0, 0, None, None, None)
    )(
        all_in[:, :NC], all_in[:, NC], all_in[:, NC + 1], at_parcel[:, :NC], at_parcel[:, NC],
        volat_a, volat_b, latent,
    )
    state_own = plane_major(jnp.where(owned_blocks, state_all, 0.0))
    state = field_major(lax.psum_scatter(state_own, "sect", scatter_dimension=0, tiled=False))
    padded = with_halo(gas_block, (("slab", 1),), 1)
    down = padded[:, :-2]
    upper = padded[:, 2:]
    flowed = plane_major(
        gas_block + 0.2 * (upper - 2.0 * gas_block + down) - 0.3 * (gas_block - down)
    )
    terms_rows = terms_all.transpose(0, 2, 1).reshape(-1, fields)
    summed = row_scatter_add(count, order, seg_sorted, terms_rows, n_cells)
    source = plane_major(summed.T.reshape(fields, width_x, width_yz))
    gas_next = plane_major(flowed + source)
    kept = jnp.where(moves[None] == 0, state, 0.0)
    from_prev = shifted(pack_slots(state, moves == 2), "slab", 1)
    from_next = shifted(pack_slots(state, moves == 1), "slab", -1)
    arrivals = jnp.concatenate([from_prev, from_next], axis=1)
    return (gas_next, kept, arrivals)


def solution(mesh):
    in_specs = (
        P(None, "slab", "sect"),
        P("slab", "sect"),
        P(None, ("sect", "slab")),
        P(("sect", "slab")),
        P(("sect", "slab")),
        P(("sect", "slab")),
        P(("sect", "slab")),
        P(),
        P(),
        P(),
    )
    out_specs = (P(None, "slab", "sect"), P(None, ("sect", "slab")), P(None, ("sect", "slab")))
    return jax.shard_map(body, mesh=mesh, in_specs=in_specs, out_specs=out_specs, check_vma=False)
```

```python
import jax
import jax.numpy as jnp
from jax import lax
from jax.experimental import pallas as pl
from jax.experimental.pallas import tpu as pltpu
from jax.experimental.layout import Layout, with_layout_constraint
from jax.sharding import PartitionSpec as P

NC = 30
RR_ITERS = 4
MOVE_CAP = 1024
UNROLL = 8


def with_halo(block, sides, width):
    for axis, dim in sides:
        count = lax.axis_size(axis)
        forward = [(i, i + 1) for i in range(count - 1)]
        backward = [(target, source) for source, target in forward]
        low = lax.ppermute(
            lax.slice_in_dim(block, block.shape[dim] - width, None, axis=dim), axis, forward
        )
        high = lax.ppermute(lax.slice_in_dim(block, 0, width, axis=dim), axis, backward)
        block = jnp.concatenate([low, block, high], axis=dim)
    return block


def shifted(shard, axis, by):
    length = lax.axis_size(axis)
    pairs = [(i, i + by) for i in range(length) if 0 <= i + by < length]
    return lax.ppermute(shard, axis, pairs)


def parcel_update(masses, drop_temp, flags, vap_p, temp_p, volat_a, volat_b, latent):
    total = jnp.sum(masses, axis=0)
    inv_total = 1.0 / total
    frac = masses * inv_total[None]
    surf = 0.5 * (drop_temp + temp_p)
    ratio = jnp.exp(volat_a[:, None] - volat_b[:, None] / surf[None])
    excess = ratio - 1.0
    weighted = frac * excess
    share = jnp.full(total.shape, 0.5, jnp.float32)
    for sweep in range(RR_ITERS):
        inv_denom = 1.0 / (1.0 + share[None] * excess)
        part = weighted * inv_denom
        residue = jnp.sum(part, axis=0)
        slope = jnp.sum(part * excess * inv_denom, axis=0) + 0.1
        share = jnp.clip(share + residue / slope, 0.02, 0.98)
    effect = flags.astype(jnp.float32) * share
    vap_eq = frac * ratio / (1.0 + effect[None] * excess)
    evap = 0.02 * total[None] * (vap_eq - vap_p)
    new_mass = masses - evap
    new_temp = (
        drop_temp
        + 0.2 * (temp_p - drop_temp)
        - 0.5 * jnp.sum(latent[:, None] * evap, axis=0) * inv_total
    )
    heat = total * (drop_temp - temp_p)
    state = jnp.concatenate([new_mass, new_temp[None]], axis=0)
    terms = jnp.concatenate([0.1 * evap, 0.05 * heat[None]], axis=0)
    return (state, terms)


def _update_kernel(in_ref, at_ref, own_ref, va_ref, vb_ref, lat_ref, state_ref, terms_ref):
    masses = in_ref[0, 0:NC, :]
    drop_temp = in_ref[0, NC:NC + 1, :]
    flags = in_ref[0, NC + 1:NC + 2, :]
    vap_p = at_ref[0, 0:NC, :]
    temp_p = at_ref[0, NC:NC + 1, :]
    own = own_ref[0] > 0.0
    total = jnp.sum(masses, axis=0, keepdims=True)
    inv_total = 1.0 / total
    frac = masses * inv_total
    surf = 0.5 * (drop_temp + temp_p)
    ratio = jnp.exp(va_ref[...] - vb_ref[...] / surf)
    excess = ratio - 1.0
    weighted = frac * excess
    share = jnp.full(total.shape, 0.5, jnp.float32)
    for sweep in range(RR_ITERS):
        inv_denom = 1.0 / (1.0 + share * excess)
        part = weighted * inv_denom
        residue = jnp.sum(part, axis=0, keepdims=True)
        slope = jnp.sum(part * excess * inv_denom, axis=0, keepdims=True) + 0.1
        share = jnp.clip(share + residue / slope, 0.02, 0.98)
    effect = flags * share
    vap_eq = frac * ratio / (1.0 + effect * excess)
    evap = 0.02 * total * (vap_eq - vap_p)
    new_temp = (
        drop_temp
        + 0.2 * (temp_p - drop_temp)
        - 0.5 * jnp.sum(lat_ref[...] * evap, axis=0, keepdims=True) * inv_total
    )
    state_ref[0, 0:NC, :] = jnp.where(own, masses - evap, 0.0)
    state_ref[0, NC:NC + 1, :] = jnp.where(own, new_temp, 0.0)
    terms_ref[0, 0:NC, :] = 0.1 * evap
    terms_ref[0, NC:NC + 1, :] = 0.05 * (total * (drop_temp - temp_p))


def owner_update(all_in, at_parcel, owned, volat_a, volat_b, latent, tile=512):
    blocks, rows_in, width = all_in.shape
    fields = at_parcel.shape[1]
    grid = (blocks, width // tile)
    column = lambda b, t: (b, 0, t)
    param = lambda b, t: (0, 0)
    out = jax.ShapeDtypeStruct((blocks, fields, width), jnp.float32)
    return pl.pallas_call(
        _update_kernel,
        grid=grid,
        in_specs=[
            pl.BlockSpec((1, rows_in, tile), column),
            pl.BlockSpec((1, fields, tile), column),
            pl.BlockSpec((1, 1, tile), column),
            pl.BlockSpec((NC, 1), param),
            pl.BlockSpec((NC, 1), param),
            pl.BlockSpec((NC, 1), param),
        ],
        out_specs=[pl.BlockSpec((1, fields, tile), column)] * 2,
        out_shape=[out, out],
    )(
        all_in, at_parcel, owned.astype(jnp.float32).reshape(blocks, 1, width),
        volat_a.reshape(NC, 1), volat_b.reshape(NC, 1), latent.reshape(NC, 1),
    )


def pack_slots(state, chosen):
    slot = jnp.where(chosen, jnp.cumsum(chosen.astype(jnp.int32)) - 1, -1)
    onehot = (slot[:, None] == jnp.arange(MOVE_CAP, dtype=jnp.int32)[None, :]).astype(jnp.bfloat16)
    high = lax.reduce_precision(state, exponent_bits=8, mantissa_bits=7)
    rest = state - high
    middle = lax.reduce_precision(rest, exponent_bits=8, mantissa_bits=7)
    low = rest - middle
    parts = jnp.concatenate([high, middle, low], axis=0).astype(jnp.bfloat16)
    out = jnp.dot(parts, onehot, preferred_element_type=jnp.float32)
    rows = state.shape[0]
    return (out[:rows] + out[rows : 2 * rows]) + out[2 * rows :]


def _gather_kernel(count_ref, dst_ref, src_ref, table_ref, out_ref):
    def step(i, carry):
        base = i * UNROLL
        for j in range(UNROLL):
            out_ref[pl.ds(dst_ref[base + j], 1), :] = table_ref[pl.ds(src_ref[base + j], 1), :]
        return carry

    lax.fori_loop(0, (count_ref[0] + UNROLL - 1) // UNROLL, step, 0)


def _scatter_kernel(count_ref, src_ref, seg_ref, rows_ref, out_ref, odd_ref):
    out_ref[...] = jnp.zeros(out_ref.shape, out_ref.dtype)
    odd_ref[...] = jnp.zeros(odd_ref.shape, odd_ref.dtype)

    def add_row(acc, k):
        acc[pl.ds(seg_ref[k], 1), :] += rows_ref[pl.ds(src_ref[k], 1), :]

    def step(i, carry):
        base = i * UNROLL
        for j in range(UNROLL):
            add_row(out_ref if j % 2 == 0 else odd_ref, base + j)
        return carry

    def rest(k, carry):
        add_row(out_ref, k)
        return carry

    full = count_ref[0] // UNROLL
    lax.fori_loop(0, full, step, 0)
    lax.fori_loop(full * UNROLL, count_ref[0], rest, 0)
    out_ref[...] += odd_ref[...]


def row_gather(count, order, local, table):
    n_out = order.shape[0]
    n_tab, width = table.shape
    spec = pltpu.PrefetchScalarGridSpec(
        num_scalar_prefetch=3,
        grid=(1,),
        in_specs=[pl.BlockSpec((n_tab, width), lambda i, *_: (0, 0))],
        out_specs=pl.BlockSpec((n_out, width), lambda i, *_: (0, 0)),
    )
    return pl.pallas_call(
        _gather_kernel,
        grid_spec=spec,
        out_shape=jax.ShapeDtypeStruct((n_out, width), table.dtype),
    )(count, order, local, table)


def row_scatter_add(count, order, seg, rows, n_cells):
    n_rows, width = rows.shape
    spec = pltpu.PrefetchScalarGridSpec(
        num_scalar_prefetch=3,
        grid=(1,),
        in_specs=[pl.BlockSpec((n_rows, width), lambda i, *_: (0, 0))],
        out_specs=pl.BlockSpec((n_cells, width), lambda i, *_: (0, 0)),
        scratch_shapes=[pltpu.VMEM((n_cells, width), jnp.float32)],
    )
    return pl.pallas_call(
        _scatter_kernel,
        grid_spec=spec,
        out_shape=jax.ShapeDtypeStruct((n_cells, width), rows.dtype),
    )(count, order, seg, rows)


def gather_sect(x):
    count = lax.axis_size("sect")
    own = lax.axis_index("sect")
    parts = [x] + [
        lax.ppermute(x, "sect", [(i, (i + k) % count) for i in range(count)])
        for k in range(1, count)
    ]
    stacked = jnp.stack(parts)
    where = (own - jnp.arange(count, dtype=jnp.int32)) % count
    return jnp.take(stacked, where, axis=0).reshape(-1)


def field_major(x):
    return with_layout_constraint(x, Layout(major_to_minor=(0, 1)))


def plane_major(x):
    return with_layout_constraint(x, Layout(major_to_minor=(0, 1, 2)))


def body(vapor, gas_temp, masses, drop_temp, cells, flags, moves, volat_a, volat_b, latent):
    gas_block = jnp.concatenate([vapor, gas_temp[None]], axis=0)
    fields, width_x, width_yz = gas_block.shape
    n_cells = width_x * width_yz
    sections = lax.axis_size("sect")
    own_sect = lax.axis_index("sect")
    plane = sections * width_yz
    parcel_in = jnp.concatenate(
        [masses, drop_temp[None], flags.astype(jnp.float32)[None]], axis=0
    )
    all_in = plane_major(lax.all_gather(field_major(parcel_in), "sect", axis=0, tiled=False))
    all_cells = gather_sect(cells)
    n_all = all_cells.shape[0]
    cell_row = all_cells // plane
    cell_col = all_cells % plane
    owned = (cell_col // width_yz) == own_sect
    local_cell = (cell_row * width_yz + cell_col % width_yz).astype(jnp.int32)
    seg = jnp.where(owned, local_cell, n_cells).astype(jnp.int32)
    position = jnp.arange(n_all, dtype=jnp.int32)
    keys = jnp.where(owned, 0, n_all).astype(jnp.int32) + position
    _, order, local_sorted, seg_sorted = lax.sort(
        (keys, position, local_cell, seg), num_keys=1
    )
    count = jnp.sum(owned.astype(jnp.int32)).reshape(1)
    table = gas_block.reshape(fields, n_cells).T
    blocks = all_in.shape[0]
    owned_blocks = owned.reshape(blocks, 1, -1)
    gathered = row_gather(count, order, local_sorted, table)
    gathered = gathered.reshape(blocks, -1, fields).transpose(0, 2, 1)
    at_parcel = plane_major(jnp.where(owned_blocks, gathered, 0.0))
    state_own, terms_all = owner_update(all_in, at_parcel, owned, volat_a, volat_b, latent)
    state = field_major(lax.psum_scatter(state_own, "sect", scatter_dimension=0, tiled=False))
    padded = with_halo(gas_block, (("slab", 1),), 1)
    down = padded[:, :-2]
    upper = padded[:, 2:]
    flowed = plane_major(
        gas_block + 0.2 * (upper - 2.0 * gas_block + down) - 0.3 * (gas_block - down)
    )
    terms_rows = terms_all.transpose(0, 2, 1).reshape(-1, fields)
    summed = row_scatter_add(count, order, seg_sorted, terms_rows, n_cells)
    source = plane_major(summed.T.reshape(fields, width_x, width_yz))
    gas_next = plane_major(flowed + source)
    kept = jnp.where(moves[None] == 0, state, 0.0)
    from_prev = shifted(pack_slots(state, moves == 2), "slab", 1)
    from_next = shifted(pack_slots(state, moves == 1), "slab", -1)
    arrivals = jnp.concatenate([from_prev, from_next], axis=1)
    return (gas_next, kept, arrivals)


def solution(mesh):
    in_specs = (
        P(None, "slab", "sect"),
        P("slab", "sect"),
        P(None, ("sect", "slab")),
        P(("sect", "slab")),
        P(("sect", "slab")),
        P(("sect", "slab")),
        P(("sect", "slab")),
        P(),
        P(),
        P(),
    )
    out_specs = (P(None, "slab", "sect"), P(None, ("sect", "slab")), P(None, ("sect", "slab")))
    return jax.shard_map(body, mesh=mesh, in_specs=in_specs, out_specs=out_specs, check_vma=False)
```

```python
import jax
import jax.numpy as jnp
from jax import lax
from jax.experimental import pallas as pl
from jax.experimental.pallas import tpu as pltpu
from jax.experimental.layout import Layout, with_layout_constraint
from jax.sharding import PartitionSpec as P

NC = 30
RR_ITERS = 4
MOVE_CAP = 1024
UNROLL = 8


def with_halo(block, sides, width):
    for axis, dim in sides:
        count = lax.axis_size(axis)
        forward = [(i, i + 1) for i in range(count - 1)]
        backward = [(target, source) for source, target in forward]
        low = lax.ppermute(
            lax.slice_in_dim(block, block.shape[dim] - width, None, axis=dim), axis, forward
        )
        high = lax.ppermute(lax.slice_in_dim(block, 0, width, axis=dim), axis, backward)
        block = jnp.concatenate([low, block, high], axis=dim)
    return block


def shifted(shard, axis, by):
    length = lax.axis_size(axis)
    pairs = [(i, i + by) for i in range(length) if 0 <= i + by < length]
    return lax.ppermute(shard, axis, pairs)


def parcel_update(masses, drop_temp, flags, vap_p, temp_p, volat_a, volat_b, latent):
    total = jnp.sum(masses, axis=0)
    inv_total = 1.0 / total
    frac = masses * inv_total[None]
    surf = 0.5 * (drop_temp + temp_p)
    ratio = jnp.exp(volat_a[:, None] - volat_b[:, None] / surf[None])
    excess = ratio - 1.0
    weighted = frac * excess
    share = jnp.full(total.shape, 0.5, jnp.float32)
    for sweep in range(RR_ITERS):
        inv_denom = 1.0 / (1.0 + share[None] * excess)
        part = weighted * inv_denom
        residue = jnp.sum(part, axis=0)
        slope = jnp.sum(part * excess * inv_denom, axis=0) + 0.1
        share = jnp.clip(share + residue / slope, 0.02, 0.98)
    effect = flags.astype(jnp.float32) * share
    vap_eq = frac * ratio / (1.0 + effect[None] * excess)
    evap = 0.02 * total[None] * (vap_eq - vap_p)
    new_mass = masses - evap
    new_temp = (
        drop_temp
        + 0.2 * (temp_p - drop_temp)
        - 0.5 * jnp.sum(latent[:, None] * evap, axis=0) * inv_total
    )
    heat = total * (drop_temp - temp_p)
    state = jnp.concatenate([new_mass, new_temp[None]], axis=0)
    terms = jnp.concatenate([0.1 * evap, 0.05 * heat[None]], axis=0)
    return (state, terms)


def pack_slots(state, chosen_sets):
    slot = jnp.full(chosen_sets[0].shape, -1, jnp.int32)
    for i, chosen in enumerate(chosen_sets):
        rank = jnp.cumsum(chosen.astype(jnp.int32)) - 1 + i * MOVE_CAP
        slot = jnp.where(chosen, rank, slot)
    columns = jnp.arange(len(chosen_sets) * MOVE_CAP, dtype=jnp.int32)
    onehot = (slot[:, None] == columns[None, :]).astype(jnp.bfloat16)
    high = lax.reduce_precision(state, exponent_bits=8, mantissa_bits=7)
    rest = state - high
    middle = lax.reduce_precision(rest, exponent_bits=8, mantissa_bits=7)
    low = rest - middle
    parts = jnp.concatenate([high, middle, low], axis=0).astype(jnp.bfloat16)
    out = jnp.dot(parts, onehot, preferred_element_type=jnp.float32)
    rows = state.shape[0]
    out = (out[:rows] + out[rows : 2 * rows]) + out[2 * rows :]
    return [out[:, i * MOVE_CAP : (i + 1) * MOVE_CAP] for i in range(len(chosen_sets))]


def _gather_kernel(count_ref, dst_ref, src_ref, table_ref, out_ref):
    def step(i, carry):
        base = i * UNROLL
        for j in range(UNROLL):
            out_ref[pl.ds(dst_ref[base + j], 1), :] = table_ref[pl.ds(src_ref[base + j], 1), :]
        return carry

    lax.fori_loop(0, (count_ref[0] + UNROLL - 1) // UNROLL, step, 0)


def _scatter_kernel(count_ref, src_ref, seg_ref, rows_ref, out_ref, odd_ref):
    out_ref[...] = jnp.zeros(out_ref.shape, out_ref.dtype)
    odd_ref[...] = jnp.zeros(odd_ref.shape, odd_ref.dtype)

    def add_row(acc, k):
        acc[pl.ds(seg_ref[k], 1), :] += rows_ref[pl.ds(src_ref[k], 1), :]

    def step(i, carry):
        base = i * UNROLL
        for j in range(UNROLL):
            add_row(out_ref if j % 2 == 0 else odd_ref, base + j)
        return carry

    def rest(k, carry):
        add_row(out_ref, k)
        return carry

    full = count_ref[0] // UNROLL
    lax.fori_loop(0, full, step, 0)
    lax.fori_loop(full * UNROLL, count_ref[0], rest, 0)
    out_ref[...] += odd_ref[...]


def row_gather(count, order, local, table):
    n_out = order.shape[0]
    n_tab, width = table.shape
    spec = pltpu.PrefetchScalarGridSpec(
        num_scalar_prefetch=3,
        grid=(1,),
        in_specs=[pl.BlockSpec((n_tab, width), lambda i, *_: (0, 0))],
        out_specs=pl.BlockSpec((n_out, width), lambda i, *_: (0, 0)),
    )
    return pl.pallas_call(
        _gather_kernel,
        grid_spec=spec,
        out_shape=jax.ShapeDtypeStruct((n_out, width), table.dtype),
    )(count, order, local, table)


def row_scatter_add(count, order, seg, rows, n_cells):
    n_rows, width = rows.shape
    spec = pltpu.PrefetchScalarGridSpec(
        num_scalar_prefetch=3,
        grid=(1,),
        in_specs=[pl.BlockSpec((n_rows, width), lambda i, *_: (0, 0))],
        out_specs=pl.BlockSpec((n_cells, width), lambda i, *_: (0, 0)),
        scratch_shapes=[pltpu.VMEM((n_cells, width), jnp.float32)],
    )
    return pl.pallas_call(
        _scatter_kernel,
        grid_spec=spec,
        out_shape=jax.ShapeDtypeStruct((n_cells, width), rows.dtype),
    )(count, order, seg, rows)


def gather_sect(x):
    count = lax.axis_size("sect")
    own = lax.axis_index("sect")
    parts = [x] + [
        lax.ppermute(x, "sect", [(i, (i + k) % count) for i in range(count)])
        for k in range(1, count)
    ]
    stacked = jnp.stack(parts)
    where = (own - jnp.arange(count, dtype=jnp.int32)) % count
    return jnp.take(stacked, where, axis=0).reshape(-1)


def field_major(x):
    return with_layout_constraint(x, Layout(major_to_minor=(0, 1)))


def plane_major(x):
    return with_layout_constraint(x, Layout(major_to_minor=(0, 1, 2)))


def body(vapor, gas_temp, masses, drop_temp, cells, flags, moves, volat_a, volat_b, latent):
    gas_block = jnp.concatenate([vapor, gas_temp[None]], axis=0)
    fields, width_x, width_yz = gas_block.shape
    n_cells = width_x * width_yz
    sections = lax.axis_size("sect")
    own_sect = lax.axis_index("sect")
    plane = sections * width_yz
    parcel_in = jnp.concatenate(
        [masses, drop_temp[None], flags.astype(jnp.float32)[None]], axis=0
    )
    all_in = plane_major(lax.all_gather(field_major(parcel_in), "sect", axis=0, tiled=False))
    all_cells = gather_sect(cells)
    n_all = all_cells.shape[0]
    cell_row = all_cells // plane
    cell_col = all_cells % plane
    owned = (cell_col // width_yz) == own_sect
    local_cell = (cell_row * width_yz + cell_col % width_yz).astype(jnp.int32)
    seg = jnp.where(owned, local_cell, n_cells).astype(jnp.int32)
    position = jnp.arange(n_all, dtype=jnp.int32)
    keys = jnp.where(owned, 0, n_all).astype(jnp.int32) + position
    _, order, local_sorted, seg_sorted = lax.sort(
        (keys, position, local_cell, seg), num_keys=1
    )
    count = jnp.sum(owned.astype(jnp.int32)).reshape(1)
    table = gas_block.reshape(fields, n_cells).T
    blocks = all_in.shape[0]
    owned_blocks = owned.reshape(blocks, 1, -1)
    gathered = row_gather(count, order, local_sorted, table)
    gathered = gathered.reshape(blocks, -1, fields).transpose(0, 2, 1)
    at_parcel = plane_major(jnp.where(owned_blocks, gathered, 0.0))
    state_all, terms_all = jax.vmap(
        parcel_update, in_axes=(0, 0, 0, 0, 0, None, None, None)
    )(
        all_in[:, :NC], all_in[:, NC], all_in[:, NC + 1], at_parcel[:, :NC], at_parcel[:, NC],
        volat_a, volat_b, latent,
    )
    state_own = plane_major(jnp.where(owned_blocks, state_all, 0.0))
    state = field_major(lax.psum_scatter(state_own, "sect", scatter_dimension=0, tiled=False))
    padded = with_halo(gas_block, (("slab", 1),), 1)
    down = padded[:, :-2]
    upper = padded[:, 2:]
    flowed = plane_major(
        gas_block + 0.2 * (upper - 2.0 * gas_block + down) - 0.3 * (gas_block - down)
    )
    terms_rows = terms_all.transpose(0, 2, 1).reshape(-1, fields)
    summed = row_scatter_add(count, order, seg_sorted, terms_rows, n_cells)
    source = plane_major(summed.T.reshape(fields, width_x, width_yz))
    gas_next = plane_major(flowed + source)
    kept = jnp.where(moves[None] == 0, state, 0.0)
    rightward, leftward = pack_slots(state, (moves == 2, moves == 1))
    from_prev = shifted(rightward, "slab", 1)
    from_next = shifted(leftward, "slab", -1)
    arrivals = jnp.concatenate([from_prev, from_next], axis=1)
    return (gas_next, kept, arrivals)


def solution(mesh):
    in_specs = (
        P(None, "slab", "sect"),
        P("slab", "sect"),
        P(None, ("sect", "slab")),
        P(("sect", "slab")),
        P(("sect", "slab")),
        P(("sect", "slab")),
        P(("sect", "slab")),
        P(),
        P(),
        P(),
    )
    out_specs = (P(None, "slab", "sect"), P(None, ("sect", "slab")), P(None, ("sect", "slab")))
    return jax.shard_map(body, mesh=mesh, in_specs=in_specs, out_specs=out_specs, check_vma=False)
```

```python
import jax
import jax.numpy as jnp
from jax import lax
from jax.experimental import pallas as pl
from jax.experimental.pallas import tpu as pltpu
from jax.experimental.layout import Layout, with_layout_constraint
from jax.sharding import PartitionSpec as P

NC = 30
RR_ITERS = 4
MOVE_CAP = 1024
UNROLL = 8


def with_halo(block, sides, width):
    for axis, dim in sides:
        count = lax.axis_size(axis)
        forward = [(i, i + 1) for i in range(count - 1)]
        backward = [(target, source) for source, target in forward]
        low = lax.ppermute(
            lax.slice_in_dim(block, block.shape[dim] - width, None, axis=dim), axis, forward
        )
        high = lax.ppermute(lax.slice_in_dim(block, 0, width, axis=dim), axis, backward)
        block = jnp.concatenate([low, block, high], axis=dim)
    return block


def shifted(shard, axis, by):
    length = lax.axis_size(axis)
    pairs = [(i, i + by) for i in range(length) if 0 <= i + by < length]
    return lax.ppermute(shard, axis, pairs)


def parcel_update(masses, drop_temp, flags, vap_p, temp_p, volat_a, volat_b, latent):
    total = jnp.sum(masses, axis=0)
    inv_total = 1.0 / total
    frac = masses * inv_total[None]
    surf = 0.5 * (drop_temp + temp_p)
    ratio = jnp.exp(volat_a[:, None] - volat_b[:, None] / surf[None])
    excess = ratio - 1.0
    weighted = frac * excess
    share = jnp.full(total.shape, 0.5, jnp.float32)
    for sweep in range(RR_ITERS):
        inv_denom = 1.0 / (1.0 + share[None] * excess)
        part = weighted * inv_denom
        residue = jnp.sum(part, axis=0)
        slope = jnp.sum(part * excess * inv_denom, axis=0) + 0.1
        share = jnp.clip(share + residue / slope, 0.02, 0.98)
    effect = flags.astype(jnp.float32) * share
    vap_eq = frac * ratio / (1.0 + effect[None] * excess)
    evap = 0.02 * total[None] * (vap_eq - vap_p)
    new_mass = masses - evap
    new_temp = (
        drop_temp
        + 0.2 * (temp_p - drop_temp)
        - 0.5 * jnp.sum(latent[:, None] * evap, axis=0) * inv_total
    )
    heat = total * (drop_temp - temp_p)
    state = jnp.concatenate([new_mass, new_temp[None]], axis=0)
    terms = jnp.concatenate([0.1 * evap, 0.05 * heat[None]], axis=0)
    return (state, terms)


def pack_slots(state, chosen_sets):
    slot = jnp.full(chosen_sets[0].shape, -1, jnp.int32)
    for i, chosen in enumerate(chosen_sets):
        rank = jnp.cumsum(chosen.astype(jnp.int32)) - 1 + i * MOVE_CAP
        slot = jnp.where(chosen, rank, slot)
    columns = jnp.arange(len(chosen_sets) * MOVE_CAP, dtype=jnp.int32)
    onehot = (slot[:, None] == columns[None, :]).astype(jnp.bfloat16)
    high = lax.reduce_precision(state, exponent_bits=8, mantissa_bits=7)
    rest = state - high
    middle = lax.reduce_precision(rest, exponent_bits=8, mantissa_bits=7)
    low = rest - middle
    parts = jnp.concatenate([high, middle, low], axis=0).astype(jnp.bfloat16)
    out = jnp.dot(parts, onehot, preferred_element_type=jnp.float32)
    rows = state.shape[0]
    out = (out[:rows] + out[rows : 2 * rows]) + out[2 * rows :]
    return [out[:, i * MOVE_CAP : (i + 1) * MOVE_CAP] for i in range(len(chosen_sets))]


def _gather_kernel(count_ref, dst_ref, src_ref, table_ref, out_ref):
    def step(i, carry):
        base = i * UNROLL
        for j in range(UNROLL):
            out_ref[pl.ds(dst_ref[base + j], 1), :] = table_ref[pl.ds(src_ref[base + j], 1), :]
        return carry

    lax.fori_loop(0, (count_ref[0] + UNROLL - 1) // UNROLL, step, 0)


def _scatter_kernel(count_ref, src_ref, seg_ref, rows_ref, out_ref, odd_ref):
    out_ref[...] = jnp.zeros(out_ref.shape, out_ref.dtype)
    odd_ref[...] = jnp.zeros(odd_ref.shape, odd_ref.dtype)

    def add_row(acc, k):
        acc[pl.ds(seg_ref[k], 1), :] += rows_ref[pl.ds(src_ref[k], 1), :]

    def step(i, carry):
        base = i * UNROLL
        for j in range(UNROLL):
            add_row(out_ref if j % 2 == 0 else odd_ref, base + j)
        return carry

    def rest(k, carry):
        add_row(out_ref, k)
        return carry

    full = count_ref[0] // UNROLL
    lax.fori_loop(0, full, step, 0)
    lax.fori_loop(full * UNROLL, count_ref[0], rest, 0)
    out_ref[...] += odd_ref[...]


def row_gather(count, order, local, table):
    n_out = order.shape[0]
    n_tab, width = table.shape
    spec = pltpu.PrefetchScalarGridSpec(
        num_scalar_prefetch=3,
        grid=(1,),
        in_specs=[pl.BlockSpec((n_tab, width), lambda i, *_: (0, 0))],
        out_specs=pl.BlockSpec((n_out, width), lambda i, *_: (0, 0)),
    )
    return pl.pallas_call(
        _gather_kernel,
        grid_spec=spec,
        out_shape=jax.ShapeDtypeStruct((n_out, width), table.dtype),
    )(count, order, local, table)


def row_scatter_add(count, order, seg, rows, n_cells):
    n_rows, width = rows.shape
    spec = pltpu.PrefetchScalarGridSpec(
        num_scalar_prefetch=3,
        grid=(1,),
        in_specs=[pl.BlockSpec((n_rows, width), lambda i, *_: (0, 0))],
        out_specs=pl.BlockSpec((n_cells, width), lambda i, *_: (0, 0)),
        scratch_shapes=[pltpu.VMEM((n_cells, width), jnp.float32)],
    )
    return pl.pallas_call(
        _scatter_kernel,
        grid_spec=spec,
        out_shape=jax.ShapeDtypeStruct((n_cells, width), rows.dtype),
    )(count, order, seg, rows)


def gather_sect(x):
    count = lax.axis_size("sect")
    own = lax.axis_index("sect")
    parts = [x] + [
        lax.ppermute(x, "sect", [(i, (i + k) % count) for i in range(count)])
        for k in range(1, count)
    ]
    stacked = jnp.stack(parts)
    where = (own - jnp.arange(count, dtype=jnp.int32)) % count
    return jnp.take(stacked, where, axis=0)


def field_major(x):
    return with_layout_constraint(x, Layout(major_to_minor=(0, 1)))


def plane_major(x):
    return with_layout_constraint(x, Layout(major_to_minor=(0, 1, 2)))


def body(vapor, gas_temp, masses, drop_temp, cells, flags, moves, volat_a, volat_b, latent):
    gas_block = jnp.concatenate([vapor, gas_temp[None]], axis=0)
    fields, width_x, width_yz = gas_block.shape
    n_cells = width_x * width_yz
    sections = lax.axis_size("sect")
    own_sect = lax.axis_index("sect")
    plane = sections * width_yz
    all_masses = plane_major(lax.all_gather(masses, "sect", axis=0, tiled=False))
    side = jnp.stack([cells.astype(jnp.float32), drop_temp, flags.astype(jnp.float32)])
    all_side = gather_sect(side)
    all_cells = all_side[:, 0].reshape(-1).astype(jnp.int32)
    n_all = all_cells.shape[0]
    cell_row = all_cells // plane
    cell_col = all_cells % plane
    owned = (cell_col // width_yz) == own_sect
    local_cell = (cell_row * width_yz + cell_col % width_yz).astype(jnp.int32)
    seg = jnp.where(owned, local_cell, n_cells).astype(jnp.int32)
    position = jnp.arange(n_all, dtype=jnp.int32)
    keys = jnp.where(owned, 0, n_all).astype(jnp.int32) + position
    _, order, local_sorted, seg_sorted = lax.sort(
        (keys, position, local_cell, seg), num_keys=1
    )
    count = jnp.sum(owned.astype(jnp.int32)).reshape(1)
    table = gas_block.reshape(fields, n_cells).T
    blocks = all_masses.shape[0]
    owned_blocks = owned.reshape(blocks, 1, -1)
    gathered = row_gather(count, order, local_sorted, table)
    gathered = gathered.reshape(blocks, -1, fields).transpose(0, 2, 1)
    at_parcel = plane_major(jnp.where(owned_blocks, gathered, 0.0))
    state_all, terms_all = jax.vmap(
        parcel_update, in_axes=(0, 0, 0, 0, 0, None, None, None)
    )(
        all_masses, all_side[:, 1], all_side[:, 2], at_parcel[:, :NC], at_parcel[:, NC],
        volat_a, volat_b, latent,
    )
    state_own = plane_major(jnp.where(owned_blocks, state_all, 0.0))
    state = field_major(lax.psum_scatter(state_own, "sect", scatter_dimension=0, tiled=False))
    padded = with_halo(gas_block, (("slab", 1),), 1)
    down = padded[:, :-2]
    upper = padded[:, 2:]
    flowed = plane_major(
        gas_block + 0.2 * (upper - 2.0 * gas_block + down) - 0.3 * (gas_block - down)
    )
    terms_rows = terms_all.transpose(0, 2, 1).reshape(-1, fields)
    summed = row_scatter_add(count, order, seg_sorted, terms_rows, n_cells)
    source = plane_major(summed.T.reshape(fields, width_x, width_yz))
    gas_next = plane_major(flowed + source)
    kept = jnp.where(moves[None] == 0, state, 0.0)
    rightward, leftward = pack_slots(state, (moves == 2, moves == 1))
    from_prev = shifted(rightward, "slab", 1)
    from_next = shifted(leftward, "slab", -1)
    arrivals = jnp.concatenate([from_prev, from_next], axis=1)
    return (gas_next, kept, arrivals)


def solution(mesh):
    in_specs = (
        P(None, "slab", "sect"),
        P("slab", "sect"),
        P(None, ("sect", "slab")),
        P(("sect", "slab")),
        P(("sect", "slab")),
        P(("sect", "slab")),
        P(("sect", "slab")),
        P(),
        P(),
        P(),
    )
    out_specs = (P(None, "slab", "sect"), P(None, ("sect", "slab")), P(None, ("sect", "slab")))
    return jax.shard_map(body, mesh=mesh, in_specs=in_specs, out_specs=out_specs, check_vma=False)
```

```python
import jax
import jax.numpy as jnp
from jax import lax
from jax.experimental import pallas as pl
from jax.experimental.pallas import tpu as pltpu
from jax.experimental.layout import Layout, with_layout_constraint
from jax.sharding import PartitionSpec as P

NC = 30
RR_ITERS = 4
MOVE_CAP = 1024
UNROLL = 8


def with_halo(block, sides, width):
    for axis, dim in sides:
        count = lax.axis_size(axis)
        forward = [(i, i + 1) for i in range(count - 1)]
        backward = [(target, source) for source, target in forward]
        low = lax.ppermute(
            lax.slice_in_dim(block, block.shape[dim] - width, None, axis=dim), axis, forward
        )
        high = lax.ppermute(lax.slice_in_dim(block, 0, width, axis=dim), axis, backward)
        block = jnp.concatenate([low, block, high], axis=dim)
    return block


def shifted(shard, axis, by):
    length = lax.axis_size(axis)
    pairs = [(i, i + by) for i in range(length) if 0 <= i + by < length]
    return lax.ppermute(shard, axis, pairs)


def parcel_update(masses, drop_temp, flags, vap_p, temp_p, volat_a, volat_b, latent):
    total = jnp.sum(masses, axis=0)
    inv_total = 1.0 / total
    frac = masses * inv_total[None]
    surf = 0.5 * (drop_temp + temp_p)
    ratio = jnp.exp(volat_a[:, None] - volat_b[:, None] / surf[None])
    excess = ratio - 1.0
    weighted = frac * excess
    share = jnp.full(total.shape, 0.5, jnp.float32)
    for sweep in range(RR_ITERS):
        inv_denom = 1.0 / (1.0 + share[None] * excess)
        part = weighted * inv_denom
        residue = jnp.sum(part, axis=0)
        slope = jnp.sum(part * excess * inv_denom, axis=0) + 0.1
        share = jnp.clip(share + residue / slope, 0.02, 0.98)
    effect = flags.astype(jnp.float32) * share
    vap_eq = frac * ratio / (1.0 + effect[None] * excess)
    evap = 0.02 * total[None] * (vap_eq - vap_p)
    new_mass = masses - evap
    new_temp = (
        drop_temp
        + 0.2 * (temp_p - drop_temp)
        - 0.5 * jnp.sum(latent[:, None] * evap, axis=0) * inv_total
    )
    heat = total * (drop_temp - temp_p)
    state = jnp.concatenate([new_mass, new_temp[None]], axis=0)
    terms = jnp.concatenate([0.1 * evap, 0.05 * heat[None]], axis=0)
    return (state, terms)


def pack_slots(state, chosen_sets):
    slot = jnp.full(chosen_sets[0].shape, -1, jnp.int32)
    for i, chosen in enumerate(chosen_sets):
        rank = jnp.cumsum(chosen.astype(jnp.int32)) - 1 + i * MOVE_CAP
        slot = jnp.where(chosen, rank, slot)
    columns = jnp.arange(len(chosen_sets) * MOVE_CAP, dtype=jnp.int32)
    onehot = (slot[:, None] == columns[None, :]).astype(jnp.bfloat16)
    high = lax.reduce_precision(state, exponent_bits=8, mantissa_bits=7)
    rest = state - high
    middle = lax.reduce_precision(rest, exponent_bits=8, mantissa_bits=7)
    low = rest - middle
    parts = jnp.concatenate([high, middle, low], axis=0).astype(jnp.bfloat16)
    out = jnp.dot(parts, onehot, preferred_element_type=jnp.float32)
    rows = state.shape[0]
    out = (out[:rows] + out[rows : 2 * rows]) + out[2 * rows :]
    return [out[:, i * MOVE_CAP : (i + 1) * MOVE_CAP] for i in range(len(chosen_sets))]


def _gather_kernel(count_ref, dst_ref, src_ref, table_ref, out_ref):
    def step(i, carry):
        base = i * UNROLL
        for j in range(UNROLL):
            out_ref[pl.ds(dst_ref[base + j], 1), :] = table_ref[pl.ds(src_ref[base + j], 1), :]
        return carry

    lax.fori_loop(0, (count_ref[0] + UNROLL - 1) // UNROLL, step, 0)


def _scatter_kernel(count_ref, src_ref, seg_ref, rows_ref, out_ref, odd_ref):
    out_ref[...] = jnp.zeros(out_ref.shape, out_ref.dtype)
    odd_ref[...] = jnp.zeros(odd_ref.shape, odd_ref.dtype)

    def add_row(acc, k):
        acc[pl.ds(seg_ref[k], 1), :] += rows_ref[pl.ds(src_ref[k], 1), :]

    def step(i, carry):
        base = i * UNROLL
        for j in range(UNROLL):
            add_row(out_ref if j % 2 == 0 else odd_ref, base + j)
        return carry

    def rest(k, carry):
        add_row(out_ref, k)
        return carry

    full = count_ref[0] // UNROLL
    lax.fori_loop(0, full, step, 0)
    lax.fori_loop(full * UNROLL, count_ref[0], rest, 0)
    out_ref[...] += odd_ref[...]


def row_gather(count, order, local, table):
    n_out = order.shape[0]
    n_tab, width = table.shape
    spec = pltpu.PrefetchScalarGridSpec(
        num_scalar_prefetch=3,
        grid=(1,),
        in_specs=[pl.BlockSpec((n_tab, width), lambda i, *_: (0, 0))],
        out_specs=pl.BlockSpec((n_out, width), lambda i, *_: (0, 0)),
    )
    return pl.pallas_call(
        _gather_kernel,
        grid_spec=spec,
        out_shape=jax.ShapeDtypeStruct((n_out, width), table.dtype),
    )(count, order, local, table)


def row_scatter_add(count, order, seg, rows, n_cells):
    n_rows, width = rows.shape
    spec = pltpu.PrefetchScalarGridSpec(
        num_scalar_prefetch=3,
        grid=(1,),
        in_specs=[pl.BlockSpec((n_rows, width), lambda i, *_: (0, 0))],
        out_specs=pl.BlockSpec((n_cells, width), lambda i, *_: (0, 0)),
        scratch_shapes=[pltpu.VMEM((n_cells, width), jnp.float32)],
    )
    return pl.pallas_call(
        _scatter_kernel,
        grid_spec=spec,
        out_shape=jax.ShapeDtypeStruct((n_cells, width), rows.dtype),
    )(count, order, seg, rows)


def gather_sect(x):
    count = lax.axis_size("sect")
    own = lax.axis_index("sect")
    parts = [x] + [
        lax.ppermute(x, "sect", [(i, (i + k) % count) for i in range(count)])
        for k in range(1, count)
    ]
    stacked = jnp.stack(parts)
    where = (own - jnp.arange(count, dtype=jnp.int32)) % count
    return jnp.take(stacked, where, axis=0)


def field_major(x):
    return with_layout_constraint(x, Layout(major_to_minor=(0, 1)))


def plane_major(x):
    return with_layout_constraint(x, Layout(major_to_minor=(0, 1, 2)))


def body(vapor, gas_temp, masses, drop_temp, cells, flags, moves, volat_a, volat_b, latent):
    gas_block = jnp.concatenate([vapor, gas_temp[None]], axis=0)
    fields, width_x, width_yz = gas_block.shape
    n_cells = width_x * width_yz
    sections = lax.axis_size("sect")
    own_sect = lax.axis_index("sect")
    plane = sections * width_yz
    all_masses = plane_major(lax.all_gather(masses, "sect", axis=0, tiled=False))
    side = jnp.stack([cells.astype(jnp.float32), drop_temp, flags.astype(jnp.float32)])
    all_side = gather_sect(side)
    all_cells = all_side[:, 0].reshape(-1).astype(jnp.int32)
    n_all = all_cells.shape[0]
    cell_row = all_cells // plane
    cell_col = all_cells % plane
    owned = (cell_col // width_yz) == own_sect
    local_cell = (cell_row * width_yz + cell_col % width_yz).astype(jnp.int32)
    seg = jnp.where(owned, local_cell, n_cells).astype(jnp.int32)
    position = jnp.arange(n_all, dtype=jnp.int32)
    keys = jnp.where(owned, 0, n_all).astype(jnp.int32) + position
    _, order, local_sorted, seg_sorted = lax.sort(
        (keys, position, local_cell, seg), num_keys=1
    )
    count = jnp.sum(owned.astype(jnp.int32)).reshape(1)
    table = gas_block.reshape(fields, n_cells).T
    blocks = all_masses.shape[0]
    owned_blocks = owned.reshape(blocks, 1, -1)
    gathered = row_gather(count, order, local_sorted, table)
    gathered = gathered.reshape(blocks, -1, fields).transpose(0, 2, 1)
    at_parcel = plane_major(jnp.where(owned_blocks, gathered, 0.0))
    state_all, terms_all = jax.vmap(
        parcel_update, in_axes=(0, 0, 0, 0, 0, None, None, None)
    )(
        all_masses, all_side[:, 1], all_side[:, 2], at_parcel[:, :NC], at_parcel[:, NC],
        volat_a, volat_b, latent,
    )
    state_own = plane_major(jnp.where(owned_blocks, state_all, 0.0))
    state = field_major(lax.psum_scatter(state_own, "sect", scatter_dimension=0, tiled=False))
    padded = with_halo(gas_block, (("slab", 1),), 1)
    down = padded[:, :-2]
    upper = padded[:, 2:]
    flowed = plane_major(
        gas_block + 0.2 * (upper - 2.0 * gas_block + down) - 0.3 * (gas_block - down)
    )
    terms_rows = terms_all.transpose(0, 2, 1).reshape(-1, fields)
    summed = row_scatter_add(count, order, seg_sorted, terms_rows, n_cells)
    source = plane_major(summed.T.reshape(fields, width_x, width_yz))
    gas_next = plane_major(flowed + source)
    kept = jnp.where(moves[None] == 0, state, 0.0)
    state_ready = state + 0.0 * gas_next[0, 0, 0]
    rightward, leftward = pack_slots(state_ready, (moves == 2, moves == 1))
    from_prev = shifted(rightward, "slab", 1)
    from_next = shifted(leftward, "slab", -1)
    arrivals = jnp.concatenate([from_prev, from_next], axis=1)
    return (gas_next, kept, arrivals)


def solution(mesh):
    in_specs = (
        P(None, "slab", "sect"),
        P("slab", "sect"),
        P(None, ("sect", "slab")),
        P(("sect", "slab")),
        P(("sect", "slab")),
        P(("sect", "slab")),
        P(("sect", "slab")),
        P(),
        P(),
        P(),
    )
    out_specs = (P(None, "slab", "sect"), P(None, ("sect", "slab")), P(None, ("sect", "slab")))
    return jax.shard_map(body, mesh=mesh, in_specs=in_specs, out_specs=out_specs, check_vma=False)
```

```python
import jax
import jax.numpy as jnp
from jax import lax
from jax.experimental import pallas as pl
from jax.experimental.pallas import tpu as pltpu
from jax.experimental.layout import Layout, with_layout_constraint
from jax.sharding import PartitionSpec as P

NC = 30
RR_ITERS = 4
MOVE_CAP = 1024
UNROLL = 8


def with_halo(block, sides, width):
    for axis, dim in sides:
        count = lax.axis_size(axis)
        forward = [(i, i + 1) for i in range(count - 1)]
        backward = [(target, source) for source, target in forward]
        low = lax.ppermute(
            lax.slice_in_dim(block, block.shape[dim] - width, None, axis=dim), axis, forward
        )
        high = lax.ppermute(lax.slice_in_dim(block, 0, width, axis=dim), axis, backward)
        block = jnp.concatenate([low, block, high], axis=dim)
    return block


def shifted(shard, axis, by):
    length = lax.axis_size(axis)
    pairs = [(i, i + by) for i in range(length) if 0 <= i + by < length]
    return lax.ppermute(shard, axis, pairs)


def parcel_update(masses, drop_temp, flags, vap_p, temp_p, volat_a, volat_b, latent):
    total = jnp.sum(masses, axis=0)
    inv_total = 1.0 / total
    frac = masses * inv_total[None]
    surf = 0.5 * (drop_temp + temp_p)
    ratio = jnp.exp(volat_a[:, None] - volat_b[:, None] / surf[None])
    excess = ratio - 1.0
    weighted = frac * excess
    share = jnp.full(total.shape, 0.5, jnp.float32)
    for sweep in range(RR_ITERS):
        inv_denom = 1.0 / (1.0 + share[None] * excess)
        part = weighted * inv_denom
        residue = jnp.sum(part, axis=0)
        slope = jnp.sum(part * excess * inv_denom, axis=0) + 0.1
        share = jnp.clip(share + residue / slope, 0.02, 0.98)
    effect = flags.astype(jnp.float32) * share
    vap_eq = frac * ratio / (1.0 + effect[None] * excess)
    evap = 0.02 * total[None] * (vap_eq - vap_p)
    new_mass = masses - evap
    new_temp = (
        drop_temp
        + 0.2 * (temp_p - drop_temp)
        - 0.5 * jnp.sum(latent[:, None] * evap, axis=0) * inv_total
    )
    heat = total * (drop_temp - temp_p)
    state = jnp.concatenate([new_mass, new_temp[None]], axis=0)
    terms = jnp.concatenate([0.1 * evap, 0.05 * heat[None]], axis=0)
    return (state, terms)


def pack_slots(state, chosen_sets):
    slot = jnp.full(chosen_sets[0].shape, -1, jnp.int32)
    for chosen in chosen_sets:
        slot = jnp.where(chosen, jnp.cumsum(chosen.astype(jnp.int32)) - 1, slot)
    onehot = (slot[:, None] == jnp.arange(MOVE_CAP, dtype=jnp.int32)[None, :]).astype(
        jnp.bfloat16
    )
    high = lax.reduce_precision(state, exponent_bits=8, mantissa_bits=7)
    rest = state - high
    middle = lax.reduce_precision(rest, exponent_bits=8, mantissa_bits=7)
    low = rest - middle
    parts = jnp.concatenate([high, middle, low], axis=0)
    picked = jnp.concatenate(
        [jnp.where(chosen[None, :], parts, 0.0) for chosen in chosen_sets], axis=0
    ).astype(jnp.bfloat16)
    out = jnp.dot(picked, onehot, preferred_element_type=jnp.float32)
    rows = state.shape[0]
    span = 3 * rows
    result = []
    for i in range(len(chosen_sets)):
        block = out[i * span : (i + 1) * span]
        result.append((block[:rows] + block[rows : 2 * rows]) + block[2 * rows :])
    return result


def _gather_kernel(count_ref, dst_ref, src_ref, table_ref, out_ref):
    def step(i, carry):
        base = i * UNROLL
        for j in range(UNROLL):
            out_ref[pl.ds(dst_ref[base + j], 1), :] = table_ref[pl.ds(src_ref[base + j], 1), :]
        return carry

    lax.fori_loop(0, (count_ref[0] + UNROLL - 1) // UNROLL, step, 0)


def _scatter_kernel(count_ref, src_ref, seg_ref, rows_ref, out_ref, odd_ref):
    out_ref[...] = jnp.zeros(out_ref.shape, out_ref.dtype)
    odd_ref[...] = jnp.zeros(odd_ref.shape, odd_ref.dtype)

    def add_row(acc, k):
        acc[pl.ds(seg_ref[k], 1), :] += rows_ref[pl.ds(src_ref[k], 1), :]

    def step(i, carry):
        base = i * UNROLL
        for j in range(UNROLL):
            add_row(out_ref if j % 2 == 0 else odd_ref, base + j)
        return carry

    def rest(k, carry):
        add_row(out_ref, k)
        return carry

    full = count_ref[0] // UNROLL
    lax.fori_loop(0, full, step, 0)
    lax.fori_loop(full * UNROLL, count_ref[0], rest, 0)
    out_ref[...] += odd_ref[...]


def row_gather(count, order, local, table):
    n_out = order.shape[0]
    n_tab, width = table.shape
    spec = pltpu.PrefetchScalarGridSpec(
        num_scalar_prefetch=3,
        grid=(1,),
        in_specs=[pl.BlockSpec((n_tab, width), lambda i, *_: (0, 0))],
        out_specs=pl.BlockSpec((n_out, width), lambda i, *_: (0, 0)),
    )
    return pl.pallas_call(
        _gather_kernel,
        grid_spec=spec,
        out_shape=jax.ShapeDtypeStruct((n_out, width), table.dtype),
    )(count, order, local, table)


def row_scatter_add(count, order, seg, rows, n_cells):
    n_rows, width = rows.shape
    spec = pltpu.PrefetchScalarGridSpec(
        num_scalar_prefetch=3,
        grid=(1,),
        in_specs=[pl.BlockSpec((n_rows, width), lambda i, *_: (0, 0))],
        out_specs=pl.BlockSpec((n_cells, width), lambda i, *_: (0, 0)),
        scratch_shapes=[pltpu.VMEM((n_cells, width), jnp.float32)],
    )
    return pl.pallas_call(
        _scatter_kernel,
        grid_spec=spec,
        out_shape=jax.ShapeDtypeStruct((n_cells, width), rows.dtype),
    )(count, order, seg, rows)


def gather_sect(x):
    count = lax.axis_size("sect")
    own = lax.axis_index("sect")
    parts = [x] + [
        lax.ppermute(x, "sect", [(i, (i + k) % count) for i in range(count)])
        for k in range(1, count)
    ]
    stacked = jnp.stack(parts)
    where = (own - jnp.arange(count, dtype=jnp.int32)) % count
    return jnp.take(stacked, where, axis=0)


def field_major(x):
    return with_layout_constraint(x, Layout(major_to_minor=(0, 1)))


def plane_major(x):
    return with_layout_constraint(x, Layout(major_to_minor=(0, 1, 2)))


def body(vapor, gas_temp, masses, drop_temp, cells, flags, moves, volat_a, volat_b, latent):
    gas_block = jnp.concatenate([vapor, gas_temp[None]], axis=0)
    fields, width_x, width_yz = gas_block.shape
    n_cells = width_x * width_yz
    sections = lax.axis_size("sect")
    own_sect = lax.axis_index("sect")
    plane = sections * width_yz
    all_masses = plane_major(lax.all_gather(masses, "sect", axis=0, tiled=False))
    side = jnp.stack([cells.astype(jnp.float32), drop_temp, flags.astype(jnp.float32)])
    all_side = gather_sect(side)
    all_cells = all_side[:, 0].reshape(-1).astype(jnp.int32)
    n_all = all_cells.shape[0]
    cell_row = all_cells // plane
    cell_col = all_cells % plane
    owned = (cell_col // width_yz) == own_sect
    local_cell = (cell_row * width_yz + cell_col % width_yz).astype(jnp.int32)
    seg = jnp.where(owned, local_cell, n_cells).astype(jnp.int32)
    position = jnp.arange(n_all, dtype=jnp.int32)
    keys = jnp.where(owned, 0, n_all).astype(jnp.int32) + position
    _, order, local_sorted, seg_sorted = lax.sort(
        (keys, position, local_cell, seg), num_keys=1
    )
    count = jnp.sum(owned.astype(jnp.int32)).reshape(1)
    table = gas_block.reshape(fields, n_cells).T
    blocks = all_masses.shape[0]
    owned_blocks = owned.reshape(blocks, 1, -1)
    gathered = row_gather(count, order, local_sorted, table)
    gathered = gathered.reshape(blocks, -1, fields).transpose(0, 2, 1)
    at_parcel = plane_major(jnp.where(owned_blocks, gathered, 0.0))
    state_all, terms_all = jax.vmap(
        parcel_update, in_axes=(0, 0, 0, 0, 0, None, None, None)
    )(
        all_masses, all_side[:, 1], all_side[:, 2], at_parcel[:, :NC], at_parcel[:, NC],
        volat_a, volat_b, latent,
    )
    state_own = plane_major(jnp.where(owned_blocks, state_all, 0.0))
    state = field_major(lax.psum_scatter(state_own, "sect", scatter_dimension=0, tiled=False))
    padded = with_halo(gas_block, (("slab", 1),), 1)
    down = padded[:, :-2]
    upper = padded[:, 2:]
    flowed = plane_major(
        gas_block + 0.2 * (upper - 2.0 * gas_block + down) - 0.3 * (gas_block - down)
    )
    terms_rows = terms_all.transpose(0, 2, 1).reshape(-1, fields)
    summed = row_scatter_add(count, order, seg_sorted, terms_rows, n_cells)
    source = plane_major(summed.T.reshape(fields, width_x, width_yz))
    gas_next = plane_major(flowed + source)
    kept = jnp.where(moves[None] == 0, state, 0.0)
    rightward, leftward = pack_slots(state, (moves == 2, moves == 1))
    from_prev = shifted(rightward, "slab", 1)
    from_next = shifted(leftward, "slab", -1)
    arrivals = jnp.concatenate([from_prev, from_next], axis=1)
    return (gas_next, kept, arrivals)


def solution(mesh):
    in_specs = (
        P(None, "slab", "sect"),
        P("slab", "sect"),
        P(None, ("sect", "slab")),
        P(("sect", "slab")),
        P(("sect", "slab")),
        P(("sect", "slab")),
        P(("sect", "slab")),
        P(),
        P(),
        P(),
    )
    out_specs = (P(None, "slab", "sect"), P(None, ("sect", "slab")), P(None, ("sect", "slab")))
    return jax.shard_map(body, mesh=mesh, in_specs=in_specs, out_specs=out_specs, check_vma=False)
```
